128 devices in a mesh: dp: 16 (over x_lo, z, core), tensor: 8 (over y, x_hi).
Axes of the slice: x: 4 (x_hi: 2, x_lo: 2; x = x_hi * 2 + x_lo), y: 4, z: 4, core: 2. Of those that a mesh axis runs over, the one named last changes fastest.
Arguments:
- tokens: bfloat16 [12288, 1024], P('dp'), may hold values from -72 to 72
- w_qkv: float32 [1024, 3072], P(('dp', 'tensor')), may hold values from -0.1875 to 0.1875
- w_out: float32 [1024, 1024], P(None, ('dp', 'tensor')), may hold values from -0.1875 to 0.1875
- w_up: float32 [1024, 4096], P(('dp', 'tensor')), may hold values from -0.1875 to 0.1875
- w_down: float32 [4096, 1024], P(None, ('dp', 'tensor')), may hold values from -0.09375 to 0.09375
- slot_request: int32 [96, 128], replicated, may hold values from -1 to 3, as said below
Outputs:
- encoded: bfloat16 [12288, 1024], P('dp')
The draws below stay inside these ranges and needn't reach their ends.
Inputs may be any that keep to these rules, and one draw needn't show every extreme that they name: `slot_request`: requests are numbered 0 to 3, all present; each request holds 1 to 48 pages and one holds exactly 48; each request's pages are full except its last page, whose empty slots are its final ones; pages may sit in any slot of the table.
All inputs are finite; a program needn't handle non-finite values.
Results may differ from the reference program's by a relative error of at most 0.025.
The reference program's roundings to bfloat16 on the way (of `qkv`, `probs`, `attn`, `first` and `inner`) count: a program that leaves them out, or rounds other values in their place, can miss the bound.
Values may be sent and summed in bfloat16 or wider, within the bound.
No kernel may reach another device: no remote copies, remote signals or barrier semaphores. Data moves between devices by JAX's collectives and lax.ppermute only.
A program may use at most 128 MiB of HBM per device.

```python
import math
import jax
import jax.numpy as jnp
from jax import lax

D = 1024
H = 16
FF = 4096
PAGE = 128
REQS = 4
PAGES = 96
MAX_PAGES = 48
TOKENS = 12288


def draw_tokens(key, part):
    base_key = jax.random.fold_in(jax.random.fold_in(key, 11), 0)
    values = jnp.clip(jax.random.normal(base_key, (TOKENS, D), jnp.float32), -6.0, 6.0)
    return values.astype(jnp.bfloat16)


def draw_slot_request(key, part):
    order_key, weight_key, tie_key, place_key, fill_key = jax.random.split(jax.random.fold_in(key, 23), 5)
    others = REQS - 1
    extra_pips = MAX_PAGES - 1
    extra = PAGES - MAX_PAGES - others
    base = jax.random.randint(weight_key, (others,), 0, 128)
    heft = base * base // 64
    section = jnp.arange(extra_pips, dtype=jnp.int32)
    ties = jax.random.permutation(tie_key, others * extra_pips).reshape(others, extra_pips)
    score = ((heft[:, None] - 24 * section[None, :]) * 4096 + ties).reshape(-1)
    ranked = jnp.argsort(jnp.argsort(-score))
    chosen = (ranked < extra).astype(jnp.int32).reshape(others, extra_pips)
    rest = 1 + jnp.sum(chosen, axis=1)
    lengths = jnp.concatenate([jnp.full((1,), MAX_PAGES, jnp.int32), rest.astype(jnp.int32)])
    lengths = lengths[jax.random.permutation(place_key, REQS)]
    ends = jnp.cumsum(lengths).astype(jnp.int32)
    page = jnp.arange(PAGES, dtype=jnp.int32)
    request = jnp.sum((page[:, None] >= ends[None, :]).astype(jnp.int32), axis=1)
    is_last = page == ends[request] - 1
    fills = jax.random.randint(fill_key, (REQS,), 1, PAGE)
    position = jnp.arange(PAGE, dtype=jnp.int32)
    live = jnp.logical_or(jnp.logical_not(is_last)[:, None], position[None, :] < fills[request][:, None])
    logical = jnp.where(live, request[:, None], -1).astype(jnp.int32)
    order = jax.random.permutation(order_key, PAGES)
    return jnp.zeros((PAGES, PAGE), jnp.int32).at[order].set(logical)


def level_of(stream_key, dims, cuts, smallest, top_value):
    level, own = 1.0, jax.random.fold_in(stream_key, 6)
    for axis_at, blocks in cuts:
        heights = jnp.exp(jax.random.uniform(jax.random.fold_in(own, axis_at), (blocks,), jnp.float32, smallest / len(cuts), top_value / len(cuts)))
        level = level * jnp.repeat(heights, dims[axis_at] // blocks).reshape([-1 if axis == axis_at else 1 for axis in range(len(dims))])
    return level


def gaussian(stream_key, extent, scale, bound, cuts=(), kind=jnp.bfloat16):
    values = jax.random.normal(stream_key, extent, jnp.float32) * scale
    if len(cuts) > 0:
        values = level_of(stream_key, extent, cuts, -0.22, 0.18) * values
    return jnp.clip(values, min=-bound, max=bound).astype(kind)


def setup_inputs(seed: int = 0) -> dict:
    key_of = jax.random.split(jax.random.key(seed), 7)
    tokens = draw_tokens(jax.random.fold_in(key_of[6], 71), 0)
    w_qkv = gaussian(key_of[1], (D, 3 * D), D ** -0.5, 0.1875, ((0, 128),), jnp.float32)
    w_out = gaussian(key_of[2], (D, D), D ** -0.5, 0.1875, ((1, 128),), jnp.float32)
    w_up = gaussian(key_of[3], (D, FF), D ** -0.5, 0.1875, ((0, 128),), jnp.float32)
    w_down = gaussian(key_of[4], (FF, D), FF ** -0.5, 0.09375, ((1, 128),), jnp.float32)
    slot_request = draw_slot_request(jax.random.fold_in(key_of[6], 71), 0)
    return dict(tokens=tokens, w_qkv=w_qkv, w_out=w_out, w_up=w_up, w_down=w_down, slot_request=slot_request)


def layer_norm(value):
    mean = lax.optimization_barrier(jnp.mean(value, axis=-1, keepdims=True))
    centred = value - mean
    spread = lax.optimization_barrier(jnp.mean(centred * centred, axis=-1, keepdims=True))
    return centred * lax.rsqrt(spread + 1e-05)

def reference(tokens, w_qkv, w_out, w_up, w_down, slot_request):
    qkv_w = w_qkv.astype(jnp.bfloat16)
    out_w = w_out.astype(jnp.bfloat16)
    up_w = w_up.astype(jnp.bfloat16)
    down_w = w_down.astype(jnp.bfloat16)
    count = tokens.shape[0]
    head_size = D // H
    qkv = jnp.dot(tokens, qkv_w, preferred_element_type=jnp.float32).astype(jnp.bfloat16)
    qkv = qkv.reshape(count, H, 3, head_size)
    queries = qkv[:, :, 0, :]
    key_rows = qkv[:, :, 1, :].astype(jnp.float32)
    value_rows = qkv[:, :, 2, :].astype(jnp.float32)
    slot_ids = slot_request.reshape(-1)
    block = math.gcd(count, 256)
    query_blocks = queries.reshape(count // block, block, H, head_size)
    id_blocks = slot_ids.reshape(count // block, block)
    scale = 1.0 / math.sqrt(head_size)

    def one_block(args):
        query_block, id_block = args
        scores = jnp.einsum('qhd,khd->hqk', query_block.astype(jnp.float32), key_rows) * scale
        allowed = (id_block[:, None] == slot_ids[None, :])[None]
        masked = jnp.where(allowed, scores, -1e+30)
        top = lax.optimization_barrier(jnp.max(masked, axis=-1, keepdims=True))
        weights = jnp.where(allowed, jnp.exp(masked - top), 0.0)
        probs = (weights / lax.optimization_barrier(jnp.sum(weights, axis=-1, keepdims=True))).astype(jnp.bfloat16)
        mixed = jnp.einsum('hqk,khd->qhd', probs.astype(jnp.float32), value_rows)
        return mixed.astype(jnp.bfloat16)
    attn = lax.map(one_block, (query_blocks, id_blocks)).reshape(count, D)
    proj = jnp.dot(attn, out_w, preferred_element_type=jnp.float32)
    first = layer_norm(tokens.astype(jnp.float32) + proj).astype(jnp.bfloat16)
    inner = jax.nn.gelu(jnp.dot(first, up_w, preferred_element_type=jnp.float32), approximate=False).astype(jnp.bfloat16)
    ffn = jnp.dot(inner, down_w, preferred_element_type=jnp.float32)
    live = (slot_ids >= 0).astype(jnp.float32)[:, None]
    encoded = layer_norm(first.astype(jnp.float32) + ffn) * live
    return encoded.astype(jnp.bfloat16)
```

```python
import math

import jax
import jax.numpy as jnp
from jax import lax
from jax.sharding import PartitionSpec as P

D = 1024
H = 16


def layer_norm(value):
    mean = jnp.mean(value, axis=-1, keepdims=True)
    centred = value - mean
    spread = jnp.mean(centred * centred, axis=-1, keepdims=True)
    return centred * lax.rsqrt(spread + 1e-05)


def row_block(weight):
    local = lax.all_to_all(weight.astype(jnp.bfloat16), "tensor", 1, 0, tiled=True)
    return lax.all_gather(local, "dp", axis=0, tiled=True)


def col_block(weight):
    local = lax.all_to_all(weight.astype(jnp.bfloat16), "tensor", 0, 1, tiled=True)
    return lax.all_gather(local, "dp", axis=1, tiled=True)


def sum_scatter(part):
    groups = lax.axis_size("tensor")
    pieces = lax.all_to_all(part.reshape(groups, -1, part.shape[1]), "tensor", 0, 0, tiled=True)
    return jnp.sum(pieces.astype(jnp.float32), axis=0)


def gather_rows(rows):
    groups = lax.axis_size("tensor")
    spread = jnp.broadcast_to(rows[None], (groups,) + rows.shape)
    return lax.all_to_all(spread, "tensor", 0, 0, tiled=True).reshape(-1, rows.shape[1])


def shards(tokens, w_qkv, w_out, w_up, w_down, slot_request):
    groups = lax.axis_size("tensor")
    tensor_rank = lax.axis_index("tensor")
    qkv_block = row_block(w_qkv)
    up_block = row_block(w_up)
    out_block = col_block(w_out)
    down_block = col_block(w_down)
    tok_rows = tokens.shape[0]
    piece_rows = tok_rows // groups
    head_size = D // H
    heads_here = qkv_block.shape[1] // (3 * head_size)
    qkv = jnp.dot(tokens, qkv_block, preferred_element_type=jnp.float32).astype(jnp.bfloat16)
    qkv = qkv.reshape(tok_rows, heads_here, 3, head_size)
    queries = qkv[:, :, 0, :]
    key_rows = qkv[:, :, 1, :].reshape(tok_rows, heads_here * head_size)
    value_rows = qkv[:, :, 2, :].reshape(tok_rows, heads_here * head_size)
    slot_ids = slot_request.reshape(-1)
    own_ids = lax.dynamic_slice_in_dim(slot_ids, lax.axis_index("dp") * tok_rows, tok_rows, 0)
    scale = 1.0 / math.sqrt(head_size)

    def update(carry, key_block, value_block, key_ids):
        running_max, total, accumulated = carry
        width = key_block.shape[0]
        key_heads = key_block.reshape(width, heads_here, head_size)
        value_heads = value_block.reshape(width, heads_here, head_size)
        scores = (
            jnp.einsum("qhd,khd->hqk", queries, key_heads, preferred_element_type=jnp.float32)
            * scale
        )
        allowed = (own_ids[:, None] == key_ids[None, :])[None]
        masked = jnp.where(allowed, scores, -1e30)
        new_max = jnp.maximum(running_max, jnp.max(masked, axis=-1))
        weights = jnp.where(allowed, jnp.exp(masked - new_max[..., None]), 0.0)
        rescale = jnp.exp(running_max - new_max)
        total = total * rescale + jnp.sum(weights, axis=-1)
        mixed = jnp.einsum(
            "hqk,khd->qhd",
            weights.astype(jnp.bfloat16),
            value_heads,
            preferred_element_type=jnp.float32,
        )
        accumulated = accumulated * jnp.transpose(rescale)[..., None] + mixed
        return (new_max, total, accumulated)

    initial = (
        jnp.full((heads_here, tok_rows), -1e30, jnp.float32),
        jnp.zeros((heads_here, tok_rows), jnp.float32),
        jnp.zeros((tok_rows, heads_here, head_size), jnp.float32),
    )
    key_piece = lax.all_gather(key_rows, "dp", axis=0, tiled=True)
    value_piece = lax.all_gather(value_rows, "dp", axis=0, tiled=True)
    key_count = key_piece.shape[0]
    steps = key_count // tok_rows
    piece_ids = slot_ids.reshape(steps, tok_rows)
    key_steps = key_piece.reshape(steps, tok_rows, key_piece.shape[1])
    value_steps = value_piece.reshape(steps, tok_rows, value_piece.shape[1])

    def one_step(state, inputs):
        key_block, value_block, key_ids = inputs
        return (update(state, key_block, value_block, key_ids), None)

    result, unused = lax.scan(one_step, initial, (key_steps, value_steps, piece_ids))
    running_max, total, accumulated = result
    attn = (
        (accumulated / jnp.transpose(total)[..., None])
        .astype(jnp.bfloat16)
        .reshape(tok_rows, heads_here * head_size)
    )
    my_rows = lax.dynamic_slice_in_dim(tokens, tensor_rank * piece_rows, piece_rows, 0)
    my_ids = lax.dynamic_slice_in_dim(own_ids, tensor_rank * piece_rows, piece_rows, 0)
    proj = sum_scatter(
        jnp.dot(attn, out_block, preferred_element_type=jnp.float32).astype(jnp.bfloat16)
    )
    first_rows = layer_norm(my_rows.astype(jnp.float32) + proj).astype(jnp.bfloat16)
    first = gather_rows(first_rows)
    inner = jax.nn.gelu(
        jnp.dot(first, up_block, preferred_element_type=jnp.float32), approximate=False
    ).astype(jnp.bfloat16)
    ffn = sum_scatter(
        jnp.dot(inner, down_block, preferred_element_type=jnp.float32).astype(jnp.bfloat16)
    )
    live = (my_ids >= 0).astype(jnp.float32)[:, None]
    encoded_rows = (layer_norm(first_rows.astype(jnp.float32) + ffn) * live).astype(jnp.bfloat16)
    return gather_rows(encoded_rows)


def solution(mesh):
    in_specs = (
        P("dp", None),
        P(("dp", "tensor"), None),
        P(None, ("dp", "tensor")),
        P(("dp", "tensor"), None),
        P(None, ("dp", "tensor")),
        P(),
    )
    out_specs = P("dp", None)
    return jax.shard_map(shards, mesh=mesh, in_specs=in_specs, out_specs=out_specs, check_vma=False)
```

```python
import math

import jax
import jax.numpy as jnp
from jax import lax
from jax.experimental import pallas as pl
from jax.experimental.pallas import tpu as pltpu
from jax.sharding import PartitionSpec as P

D = 1024
H = 16


def layer_norm(value):
    mean = jnp.mean(value, axis=-1, keepdims=True)
    centred = value - mean
    spread = jnp.mean(centred * centred, axis=-1, keepdims=True)
    return centred * lax.rsqrt(spread + 1e-05)


def row_block(weight):
    local = lax.all_to_all(weight.astype(jnp.bfloat16), "tensor", 1, 0, tiled=True)
    return lax.all_gather(local, "dp", axis=0, tiled=True)


def col_block(weight):
    local = lax.all_to_all(weight.astype(jnp.bfloat16), "tensor", 0, 1, tiled=True)
    return lax.all_gather(local, "dp", axis=1, tiled=True)


def sum_scatter(part):
    groups = lax.axis_size("tensor")
    pieces = lax.all_to_all(part.reshape(groups, -1, part.shape[1]), "tensor", 0, 0, tiled=True)
    return jnp.sum(pieces.astype(jnp.float32), axis=0)


def gather_rows(rows):
    groups = lax.axis_size("tensor")
    spread = jnp.broadcast_to(rows[None], (groups,) + rows.shape)
    return lax.all_to_all(spread, "tensor", 0, 0, tiled=True).reshape(-1, rows.shape[1])


HEAD = D // H
INTERPRET = False


def attention_kernel(allowed_ref, q_ref, qid_ref, k_ref, v_ref, kid_ref, o_ref, m_ref, l_ref, acc_ref):
    i = pl.program_id(0)
    pages = k_ref.shape[0]
    heads = q_ref.shape[1] // HEAD
    scale = 1.0 / math.sqrt(HEAD)
    q = q_ref[...]
    lane_head = lax.broadcasted_iota(jnp.int32, q.shape, 1) // HEAD
    head_q = [jnp.where(lane_head == h, q, jnp.zeros_like(q)) for h in range(heads)]
    qid = qid_ref[...]
    m_ref[...] = jnp.full(m_ref.shape, -1e30, jnp.float32)
    l_ref[...] = jnp.zeros(l_ref.shape, jnp.float32)
    acc_ref[...] = jnp.zeros(acc_ref.shape, jnp.float32)

    def visit(kp):
        k = k_ref[kp]
        v = v_ref[kp]
        allowed = qid == kid_ref[kp]
        for h in range(heads):
            s = lax.dot_general(
                head_q[h], k, (((1,), (1,)), ((), ())), preferred_element_type=jnp.float32
            ) * scale
            s = jnp.where(allowed, s, -1e30)
            m_old = m_ref[h]
            m_new = jnp.maximum(m_old, jnp.max(s, axis=1, keepdims=True))
            p = jnp.where(allowed, jnp.exp(s - m_new), 0.0)
            alpha = jnp.exp(m_old - m_new)
            l_ref[h] = alpha * l_ref[h] + jnp.sum(p, axis=1, keepdims=True)
            acc_ref[h] = alpha * acc_ref[h] + jnp.dot(
                p.astype(jnp.bfloat16), v, preferred_element_type=jnp.float32
            )
            m_ref[h] = m_new

    def body(kp, carry):
        @pl.when(allowed_ref[i * pages + kp] > 0)
        def _():
            visit(kp)

        return carry

    lax.fori_loop(0, pages, body, 0)
    out = acc_ref[0] / l_ref[0]
    for h in range(1, heads):
        out = jnp.where(lane_head == h, acc_ref[h] / l_ref[h], out)
    o_ref[...] = out.astype(o_ref.dtype)


def paged_attention(queries, keys, values, slot_request, dp_rank):
    pages, page = slot_request.shape
    rows, width = queries.shape
    own_pages = rows // page
    heads = width // HEAD
    present = (
        slot_request[:, :, None] == jnp.arange(-1, 4, dtype=jnp.int32)[None, None, :]
    ).any(axis=1).astype(jnp.float32)
    own = lax.dynamic_slice_in_dim(present, dp_rank * own_pages, own_pages, 0)
    allowed = (jnp.dot(own, present.T) > 0).astype(jnp.int32).reshape(-1)
    own_ids = lax.dynamic_slice_in_dim(slot_request, dp_rank * own_pages, own_pages, 0)
    qid = own_ids.reshape(rows, 1)
    kid = slot_request.reshape(pages, 1, page)
    k3 = keys.reshape(pages, page, width)
    v3 = values.reshape(pages, page, width)
    grid_spec = pltpu.PrefetchScalarGridSpec(
        num_scalar_prefetch=1,
        grid=(own_pages,),
        in_specs=[
            pl.BlockSpec((page, width), lambda i, a: (i, 0)),
            pl.BlockSpec((page, 1), lambda i, a: (i, 0)),
            pl.BlockSpec((pages, page, width), lambda i, a: (0, 0, 0)),
            pl.BlockSpec((pages, page, width), lambda i, a: (0, 0, 0)),
            pl.BlockSpec((pages, 1, page), lambda i, a: (0, 0, 0)),
        ],
        out_specs=pl.BlockSpec((page, width), lambda i, a: (i, 0)),
        scratch_shapes=[
            pltpu.VMEM((heads, page, 1), jnp.float32),
            pltpu.VMEM((heads, page, 1), jnp.float32),
            pltpu.VMEM((heads, page, width), jnp.float32),
        ],
    )
    return pl.pallas_call(
        attention_kernel,
        grid_spec=grid_spec,
        out_shape=jax.ShapeDtypeStruct((rows, width), jnp.bfloat16),
        interpret=INTERPRET,
    )(allowed, queries, qid, k3, v3, kid)


def shards(tokens, w_qkv, w_out, w_up, w_down, slot_request):
    groups = lax.axis_size("tensor")
    tensor_rank = lax.axis_index("tensor")
    qkv_block = row_block(w_qkv)
    up_block = row_block(w_up)
    out_block = col_block(w_out)
    down_block = col_block(w_down)
    tok_rows = tokens.shape[0]
    piece_rows = tok_rows // groups
    head_size = D // H
    heads_here = qkv_block.shape[1] // (3 * head_size)
    qkv = jnp.dot(tokens, qkv_block, preferred_element_type=jnp.float32).astype(jnp.bfloat16)
    qkv = qkv.reshape(tok_rows, heads_here, 3, head_size)
    queries = qkv[:, :, 0, :]
    key_rows = qkv[:, :, 1, :].reshape(tok_rows, heads_here * head_size)
    value_rows = qkv[:, :, 2, :].reshape(tok_rows, heads_here * head_size)
    slot_ids = slot_request.reshape(-1)
    own_ids = lax.dynamic_slice_in_dim(slot_ids, lax.axis_index("dp") * tok_rows, tok_rows, 0)

    key_piece = lax.all_gather(key_rows, "dp", axis=0, tiled=True)
    value_piece = lax.all_gather(value_rows, "dp", axis=0, tiled=True)
    attn = paged_attention(
        queries.reshape(tok_rows, heads_here * head_size),
        key_piece,
        value_piece,
        slot_request,
        lax.axis_index("dp"),
    )
    my_rows = lax.dynamic_slice_in_dim(tokens, tensor_rank * piece_rows, piece_rows, 0)
    my_ids = lax.dynamic_slice_in_dim(own_ids, tensor_rank * piece_rows, piece_rows, 0)
    proj = sum_scatter(
        jnp.dot(attn, out_block, preferred_element_type=jnp.float32).astype(jnp.bfloat16)
    )
    first_rows = layer_norm(my_rows.astype(jnp.float32) + proj).astype(jnp.bfloat16)
    first = gather_rows(first_rows)
    inner = jax.nn.gelu(
        jnp.dot(first, up_block, preferred_element_type=jnp.float32), approximate=False
    ).astype(jnp.bfloat16)
    ffn = sum_scatter(
        jnp.dot(inner, down_block, preferred_element_type=jnp.float32).astype(jnp.bfloat16)
    )
    live = (my_ids >= 0).astype(jnp.float32)[:, None]
    encoded_rows = (layer_norm(first_rows.astype(jnp.float32) + ffn) * live).astype(jnp.bfloat16)
    return gather_rows(encoded_rows)


def solution(mesh):
    in_specs = (
        P("dp", None),
        P(("dp", "tensor"), None),
        P(None, ("dp", "tensor")),
        P(("dp", "tensor"), None),
        P(None, ("dp", "tensor")),
        P(),
    )
    out_specs = P("dp", None)
    return jax.shard_map(shards, mesh=mesh, in_specs=in_specs, out_specs=out_specs, check_vma=False)
```

```python
import math

import jax
import jax.numpy as jnp
from jax import lax
from jax.experimental import pallas as pl
from jax.experimental.pallas import tpu as pltpu
from jax.sharding import PartitionSpec as P

D = 1024
H = 16


def layer_norm(value):
    mean = jnp.mean(value, axis=-1, keepdims=True)
    centred = value - mean
    spread = jnp.mean(centred * centred, axis=-1, keepdims=True)
    return centred * lax.rsqrt(spread + 1e-05)


def row_block(weight):
    local = lax.all_to_all(weight.astype(jnp.bfloat16), "tensor", 1, 0, tiled=True)
    return lax.all_gather(local, "dp", axis=0, tiled=True)


def col_block(weight):
    local = lax.all_to_all(weight.astype(jnp.bfloat16), "tensor", 0, 1, tiled=True)
    return lax.all_gather(local, "dp", axis=1, tiled=True)


def sum_scatter(part):
    groups = lax.axis_size("tensor")
    pieces = lax.all_to_all(part.reshape(groups, -1, part.shape[1]), "tensor", 0, 0, tiled=True)
    return jnp.sum(pieces.astype(jnp.float32), axis=0)


def gather_rows(rows):
    groups = lax.axis_size("tensor")
    spread = jnp.broadcast_to(rows[None], (groups,) + rows.shape)
    return lax.all_to_all(spread, "tensor", 0, 0, tiled=True).reshape(-1, rows.shape[1])


HEAD = D // H
INTERPRET = False
CHUNK = 4


def attention_kernel(list_ref, count_ref, q_ref, qid_ref, kt_ref, v_ref, kid_ref, o_ref, m_ref, l_ref, acc_ref):
    i = pl.program_id(0)
    pages = kt_ref.shape[0]
    page = kt_ref.shape[2]
    heads = q_ref.shape[1] // HEAD
    scale = 1.0 / math.sqrt(HEAD)
    q = q_ref[...]
    lane_head = lax.broadcasted_iota(jnp.int32, q.shape, 1) // HEAD
    head_q = [jnp.where(lane_head == h, q, jnp.zeros_like(q)) for h in range(heads)]
    qid = qid_ref[...]
    count = count_ref[i]
    m_ref[...] = jnp.full(m_ref.shape, -1e30, jnp.float32)
    l_ref[...] = jnp.zeros(l_ref.shape, jnp.float32)
    acc_ref[...] = jnp.zeros(acc_ref.shape, jnp.float32)
    slot_chunk = lax.broadcasted_iota(jnp.int32, (1, CHUNK * page), 1) // page

    def body(c, carry):
        base = c * CHUNK
        kps = [list_ref[i * (pages + CHUNK) + base + j] for j in range(CHUNK)]
        kt = jnp.concatenate([kt_ref[kp] for kp in kps], axis=1)
        v = jnp.concatenate([v_ref[kp] for kp in kps], axis=0)
        kid = jnp.concatenate([kid_ref[kp] for kp in kps], axis=1)
        allowed = jnp.logical_and(qid == kid, slot_chunk + base < count)
        for h in range(heads):
            s = jnp.dot(head_q[h], kt, preferred_element_type=jnp.float32) * scale
            s = jnp.where(allowed, s, -1e30)
            m_old = m_ref[h]
            m_new = jnp.maximum(m_old, jnp.max(s, axis=1, keepdims=True))
            p = jnp.where(allowed, jnp.exp(s - m_new), 0.0)
            alpha = jnp.exp(m_old - m_new)
            l_ref[h] = alpha * l_ref[h] + jnp.sum(p, axis=1, keepdims=True)
            acc_ref[h] = alpha * acc_ref[h] + jnp.dot(
                p.astype(jnp.bfloat16), v, preferred_element_type=jnp.float32
            )
            m_ref[h] = m_new
        return carry

    lax.fori_loop(0, (count + CHUNK - 1) // CHUNK, body, 0)
    out = acc_ref[0] / l_ref[0]
    for h in range(1, heads):
        out = jnp.where(lane_head == h, acc_ref[h] / l_ref[h], out)
    o_ref[...] = out.astype(o_ref.dtype)


def paged_attention(queries, keys, values, slot_request, dp_rank):
    pages, page = slot_request.shape
    rows, width = queries.shape
    own_pages = rows // page
    heads = width // HEAD
    present = (
        slot_request[:, :, None] == jnp.arange(-1, 4, dtype=jnp.int32)[None, None, :]
    ).any(axis=1).astype(jnp.float32)
    own = lax.dynamic_slice_in_dim(present, dp_rank * own_pages, own_pages, 0)
    allowed = (jnp.dot(own, present.T) > 0).astype(jnp.int32)
    counts = jnp.sum(allowed, axis=1)
    visit = jnp.argsort(1 - allowed, axis=1, stable=True).astype(jnp.int32)
    visit = jnp.pad(visit, ((0, 0), (0, CHUNK)), mode="edge").reshape(-1)
    own_ids = lax.dynamic_slice_in_dim(slot_request, dp_rank * own_pages, own_pages, 0)
    qid = own_ids.reshape(rows, 1)
    kid = slot_request.reshape(pages, 1, page)
    kt3 = jnp.transpose(keys.reshape(pages, page, width), (0, 2, 1))
    v3 = values.reshape(pages, page, width)
    grid_spec = pltpu.PrefetchScalarGridSpec(
        num_scalar_prefetch=2,
        grid=(own_pages,),
        in_specs=[
            pl.BlockSpec((page, width), lambda i, a, n: (i, 0)),
            pl.BlockSpec((page, 1), lambda i, a, n: (i, 0)),
            pl.BlockSpec((pages, width, page), lambda i, a, n: (0, 0, 0)),
            pl.BlockSpec((pages, page, width), lambda i, a, n: (0, 0, 0)),
            pl.BlockSpec((pages, 1, page), lambda i, a, n: (0, 0, 0)),
        ],
        out_specs=pl.BlockSpec((page, width), lambda i, a, n: (i, 0)),
        scratch_shapes=[
            pltpu.VMEM((heads, page, 1), jnp.float32),
            pltpu.VMEM((heads, page, 1), jnp.float32),
            pltpu.VMEM((heads, page, width), jnp.float32),
        ],
    )
    return pl.pallas_call(
        attention_kernel,
        grid_spec=grid_spec,
        out_shape=jax.ShapeDtypeStruct((rows, width), jnp.bfloat16),
        interpret=INTERPRET,
    )(visit, counts, queries, qid, kt3, v3, kid)


def shards(tokens, w_qkv, w_out, w_up, w_down, slot_request):
    groups = lax.axis_size("tensor")
    tensor_rank = lax.axis_index("tensor")
    qkv_block = row_block(w_qkv)
    up_block = row_block(w_up)
    out_block = col_block(w_out)
    down_block = col_block(w_down)
    tok_rows = tokens.shape[0]
    piece_rows = tok_rows // groups
    head_size = D // H
    heads_here = qkv_block.shape[1] // (3 * head_size)
    qkv = jnp.dot(tokens, qkv_block, preferred_element_type=jnp.float32).astype(jnp.bfloat16)
    qkv = qkv.reshape(tok_rows, heads_here, 3, head_size)
    queries = qkv[:, :, 0, :]
    key_rows = qkv[:, :, 1, :].reshape(tok_rows, heads_here * head_size)
    value_rows = qkv[:, :, 2, :].reshape(tok_rows, heads_here * head_size)
    slot_ids = slot_request.reshape(-1)
    own_ids = lax.dynamic_slice_in_dim(slot_ids, lax.axis_index("dp") * tok_rows, tok_rows, 0)

    key_piece = lax.all_gather(key_rows, "dp", axis=0, tiled=True)
    value_piece = lax.all_gather(value_rows, "dp", axis=0, tiled=True)
    key_piece, value_piece, up_block, down_block = lax.optimization_barrier(
        (key_piece, value_piece, up_block, down_block)
    )
    attn = paged_attention(
        queries.reshape(tok_rows, heads_here * head_size),
        key_piece,
        value_piece,
        slot_request,
        lax.axis_index("dp"),
    )
    my_rows = lax.dynamic_slice_in_dim(tokens, tensor_rank * piece_rows, piece_rows, 0)
    my_ids = lax.dynamic_slice_in_dim(own_ids, tensor_rank * piece_rows, piece_rows, 0)
    proj = sum_scatter(
        jnp.dot(attn, out_block, preferred_element_type=jnp.float32).astype(jnp.bfloat16)
    )
    first_rows = layer_norm(my_rows.astype(jnp.float32) + proj).astype(jnp.bfloat16)
    first = gather_rows(first_rows)
    inner = jax.nn.gelu(
        jnp.dot(first, up_block, preferred_element_type=jnp.float32), approximate=False
    ).astype(jnp.bfloat16)
    ffn = sum_scatter(
        jnp.dot(inner, down_block, preferred_element_type=jnp.float32).astype(jnp.bfloat16)
    )
    live = (my_ids >= 0).astype(jnp.float32)[:, None]
    encoded_rows = (layer_norm(first_rows.astype(jnp.float32) + ffn) * live).astype(jnp.bfloat16)
    return gather_rows(encoded_rows)


def solution(mesh):
    in_specs = (
        P("dp", None),
        P(("dp", "tensor"), None),
        P(None, ("dp", "tensor")),
        P(("dp", "tensor"), None),
        P(None, ("dp", "tensor")),
        P(),
    )
    out_specs = P("dp", None)
    return jax.shard_map(shards, mesh=mesh, in_specs=in_specs, out_specs=out_specs, check_vma=False)
```

```python
import math

import jax
import jax.numpy as jnp
from jax import lax
from jax.experimental import pallas as pl
from jax.experimental.pallas import tpu as pltpu
from jax.sharding import PartitionSpec as P

D = 1024
H = 16


def layer_norm(value):
    mean = jnp.mean(value, axis=-1, keepdims=True)
    centred = value - mean
    spread = jnp.mean(centred * centred, axis=-1, keepdims=True)
    return centred * lax.rsqrt(spread + 1e-05)


def spread_weights(w_qkv, w_out, w_up, w_down):
    groups = lax.axis_size("tensor")
    qkv = w_qkv.astype(jnp.bfloat16)
    up = w_up.astype(jnp.bfloat16)
    out = w_out.astype(jnp.bfloat16)
    down = w_down.astype(jnp.bfloat16)
    rows = qkv.shape[0]
    parts = [
        qkv.reshape(rows, groups, -1).transpose(1, 0, 2).reshape(groups, -1),
        up.reshape(rows, groups, -1).transpose(1, 0, 2).reshape(groups, -1),
        down.reshape(groups, -1),
        jnp.broadcast_to(out.reshape(1, -1), (groups, out.size)),
    ]
    sizes = [p.shape[1] for p in parts]
    got = lax.all_to_all(jnp.concatenate(parts, axis=1), "tensor", 0, 0, tiled=True)
    cut = [sum(sizes[:k]) for k in range(5)]
    piece = [got[:, cut[k]:cut[k + 1]] for k in range(4)]
    qkv_local = piece[0].reshape(groups * rows, -1)
    up_local = piece[1].reshape(groups * rows, -1)
    down_rows = down.shape[0] // groups
    down_local = piece[2].reshape(groups, down_rows, -1).transpose(1, 0, 2).reshape(down_rows, -1)
    out_local = piece[3].reshape(groups, out.shape[0], -1).transpose(1, 0, 2).reshape(out.shape[0], -1)
    qkv_block = lax.all_gather(qkv_local, "dp", axis=0, tiled=True)
    rest = [up_local, down_local, out_local]
    flat = jnp.concatenate([r.reshape(-1) for r in rest])
    all_flat = lax.all_gather(flat, "dp", axis=0, tiled=False)
    dp_size = all_flat.shape[0]
    offs = [0, up_local.size, up_local.size + down_local.size, flat.shape[0]]
    up_block = all_flat[:, offs[0]:offs[1]].reshape(dp_size * up_local.shape[0], -1)
    down_block = (
        all_flat[:, offs[1]:offs[2]].reshape(dp_size, *down_local.shape).transpose(1, 0, 2).reshape(down_rows, -1)
    )
    out_full = (
        all_flat[:, offs[2]:offs[3]].reshape(dp_size, *out_local.shape).transpose(1, 0, 2).reshape(out.shape[0], -1)
    )
    return qkv_block, up_block, down_block, out_full


def sum_scatter(part):
    groups = lax.axis_size("tensor")
    pieces = lax.all_to_all(part.reshape(groups, -1, part.shape[1]), "tensor", 0, 0, tiled=True)
    return jnp.sum(pieces.astype(jnp.float32), axis=0)


def gather_rows(rows):
    groups = lax.axis_size("tensor")
    spread = jnp.broadcast_to(rows[None], (groups,) + rows.shape)
    return lax.all_to_all(spread, "tensor", 0, 0, tiled=True).reshape(-1, rows.shape[1])


HEAD = D // H
INTERPRET = False
CHUNK = 4


def attention_kernel(list_ref, count_ref, q_ref, qid_ref, kt_ref, v_ref, kid_ref, o_ref, m_ref, l_ref, acc_ref):
    i = pl.program_id(0)
    pages = kt_ref.shape[0]
    page = kt_ref.shape[2]
    heads = q_ref.shape[1] // HEAD
    scale = 1.0 / math.sqrt(HEAD)
    q = q_ref[...]
    lane_head = lax.broadcasted_iota(jnp.int32, q.shape, 1) // HEAD
    head_q = [jnp.where(lane_head == h, q, jnp.zeros_like(q)) for h in range(heads)]
    qid = qid_ref[...]
    count = count_ref[i]
    m_ref[...] = jnp.full(m_ref.shape, -1e30, jnp.float32)
    l_ref[...] = jnp.zeros(l_ref.shape, jnp.float32)
    acc_ref[...] = jnp.zeros(acc_ref.shape, jnp.float32)
    slot_chunk = lax.broadcasted_iota(jnp.int32, (1, CHUNK * page), 1) // page

    def body(c, carry):
        base = c * CHUNK
        kps = [list_ref[i * (pages + CHUNK) + base + j] for j in range(CHUNK)]
        kt = jnp.concatenate([kt_ref[kp] for kp in kps], axis=1)
        v = jnp.concatenate([v_ref[kp] for kp in kps], axis=0)
        kid = jnp.concatenate([kid_ref[kp] for kp in kps], axis=1)
        allowed = jnp.logical_and(qid == kid, slot_chunk + base < count)
        for h in range(heads):
            s = jnp.dot(head_q[h], kt, preferred_element_type=jnp.float32) * scale
            s = jnp.where(allowed, s, -1e30)
            m_old = m_ref[h]
            m_new = jnp.maximum(m_old, jnp.max(s, axis=1, keepdims=True))
            p = jnp.where(allowed, jnp.exp(s - m_new), 0.0)
            alpha = jnp.exp(m_old - m_new)
            l_ref[h] = alpha * l_ref[h] + jnp.sum(p, axis=1, keepdims=True)
            acc_ref[h] = alpha * acc_ref[h] + jnp.dot(
                p.astype(jnp.bfloat16), v, preferred_element_type=jnp.float32
            )
            m_ref[h] = m_new
        return carry

    lax.fori_loop(0, (count + CHUNK - 1) // CHUNK, body, 0)
    out = acc_ref[0] / l_ref[0]
    for h in range(1, heads):
        out = jnp.where(lane_head == h, acc_ref[h] / l_ref[h], out)
    o_ref[...] = out.astype(o_ref.dtype)


def paged_attention(queries, keys, values, slot_request, dp_rank):
    pages, page = slot_request.shape
    rows, width = queries.shape
    own_pages = rows // page
    heads = width // HEAD
    present = (
        slot_request[:, :, None] == jnp.arange(-1, 4, dtype=jnp.int32)[None, None, :]
    ).any(axis=1).astype(jnp.float32)
    own = lax.dynamic_slice_in_dim(present, dp_rank * own_pages, own_pages, 0)
    allowed = (jnp.dot(own, present.T) > 0).astype(jnp.int32)
    counts = jnp.sum(allowed, axis=1)
    visit = jnp.argsort(1 - allowed, axis=1, stable=True).astype(jnp.int32)
    visit = jnp.pad(visit, ((0, 0), (0, CHUNK)), mode="edge").reshape(-1)
    own_ids = lax.dynamic_slice_in_dim(slot_request, dp_rank * own_pages, own_pages, 0)
    qid = own_ids.reshape(rows, 1)
    kid = slot_request.reshape(pages, 1, page)
    kt3 = jnp.transpose(keys.reshape(pages, page, width), (0, 2, 1))
    v3 = values.reshape(pages, page, width)
    grid_spec = pltpu.PrefetchScalarGridSpec(
        num_scalar_prefetch=2,
        grid=(own_pages,),
        in_specs=[
            pl.BlockSpec((page, width), lambda i, a, n: (i, 0)),
            pl.BlockSpec((page, 1), lambda i, a, n: (i, 0)),
            pl.BlockSpec((pages, width, page), lambda i, a, n: (0, 0, 0)),
            pl.BlockSpec((pages, page, width), lambda i, a, n: (0, 0, 0)),
            pl.BlockSpec((pages, 1, page), lambda i, a, n: (0, 0, 0)),
        ],
        out_specs=pl.BlockSpec((page, width), lambda i, a, n: (i, 0)),
        scratch_shapes=[
            pltpu.VMEM((heads, page, 1), jnp.float32),
            pltpu.VMEM((heads, page, 1), jnp.float32),
            pltpu.VMEM((heads, page, width), jnp.float32),
        ],
    )
    return pl.pallas_call(
        attention_kernel,
        grid_spec=grid_spec,
        out_shape=jax.ShapeDtypeStruct((rows, width), jnp.bfloat16),
        interpret=INTERPRET,
    )(visit, counts, queries, qid, kt3, v3, kid)


def shards(tokens, w_qkv, w_out, w_up, w_down, slot_request):
    groups = lax.axis_size("tensor")
    tensor_rank = lax.axis_index("tensor")
    qkv_block, up_block, down_block, out_full = spread_weights(w_qkv, w_out, w_up, w_down)
    tok_rows = tokens.shape[0]
    piece_rows = tok_rows // groups
    head_size = D // H
    heads_here = qkv_block.shape[1] // (3 * head_size)
    qkv = jnp.dot(tokens, qkv_block, preferred_element_type=jnp.float32).astype(jnp.bfloat16)
    qkv = qkv.reshape(tok_rows, heads_here, 3, head_size)
    queries = qkv[:, :, 0, :]
    key_rows = qkv[:, :, 1, :].reshape(tok_rows, heads_here * head_size)
    value_rows = qkv[:, :, 2, :].reshape(tok_rows, heads_here * head_size)
    slot_ids = slot_request.reshape(-1)
    own_ids = lax.dynamic_slice_in_dim(slot_ids, lax.axis_index("dp") * tok_rows, tok_rows, 0)

    key_piece = lax.all_gather(key_rows, "dp", axis=0, tiled=True)
    value_piece = lax.all_gather(value_rows, "dp", axis=0, tiled=True)
    key_piece, value_piece, up_block, down_block, out_full = lax.optimization_barrier(
        (key_piece, value_piece, up_block, down_block, out_full)
    )
    attn = paged_attention(
        queries.reshape(tok_rows, heads_here * head_size),
        key_piece,
        value_piece,
        slot_request,
        lax.axis_index("dp"),
    )
    my_rows = lax.dynamic_slice_in_dim(tokens, tensor_rank * piece_rows, piece_rows, 0)
    my_ids = lax.dynamic_slice_in_dim(own_ids, tensor_rank * piece_rows, piece_rows, 0)
    heads_rows = lax.all_to_all(attn.reshape(groups, piece_rows, -1), "tensor", 0, 0, tiled=True)
    heads_rows = heads_rows.transpose(1, 0, 2).reshape(piece_rows, -1)
    proj = jnp.dot(heads_rows, out_full, preferred_element_type=jnp.float32)
    first_rows = layer_norm(my_rows.astype(jnp.float32) + proj).astype(jnp.bfloat16)
    first = gather_rows(first_rows)
    inner = jax.nn.gelu(
        jnp.dot(first, up_block, preferred_element_type=jnp.float32), approximate=False
    ).astype(jnp.bfloat16)
    ffn = sum_scatter(
        jnp.dot(inner, down_block, preferred_element_type=jnp.float32).astype(jnp.bfloat16)
    )
    live = (my_ids >= 0).astype(jnp.float32)[:, None]
    encoded_rows = (layer_norm(first_rows.astype(jnp.float32) + ffn) * live).astype(jnp.bfloat16)
    return gather_rows(encoded_rows)


def solution(mesh):
    in_specs = (
        P("dp", None),
        P(("dp", "tensor"), None),
        P(None, ("dp", "tensor")),
        P(("dp", "tensor"), None),
        P(None, ("dp", "tensor")),
        P(),
    )
    out_specs = P("dp", None)
    return jax.shard_map(shards, mesh=mesh, in_specs=in_specs, out_specs=out_specs, check_vma=False)
```

```python
import math

import jax
import jax.numpy as jnp
from jax import lax
from jax.experimental import pallas as pl
from jax.experimental.pallas import tpu as pltpu
from jax.sharding import PartitionSpec as P

D = 1024
H = 16


def layer_norm(value):
    mean = jnp.mean(value, axis=-1, keepdims=True)
    centred = value - mean
    spread = jnp.mean(centred * centred, axis=-1, keepdims=True)
    return centred * lax.rsqrt(spread + 1e-05)


def spread_weights(w_qkv, w_out, w_up, w_down):
    groups = lax.axis_size("tensor")
    qkv = w_qkv.astype(jnp.bfloat16)
    up = w_up.astype(jnp.bfloat16)
    out = w_out.astype(jnp.bfloat16)
    down = w_down.astype(jnp.bfloat16)
    rows = qkv.shape[0]
    parts = [
        qkv.reshape(rows, groups, -1).transpose(1, 0, 2).reshape(groups, -1),
        up.reshape(rows, groups, -1).transpose(1, 0, 2).reshape(groups, -1),
        down.reshape(groups, -1),
        jnp.broadcast_to(out.reshape(1, -1), (groups, out.size)),
    ]
    sizes = [p.shape[1] for p in parts]
    got = lax.all_to_all(jnp.concatenate(parts, axis=1), "tensor", 0, 0, tiled=True)
    cut = [sum(sizes[:k]) for k in range(5)]
    piece = [got[:, cut[k]:cut[k + 1]] for k in range(4)]
    qkv_local = piece[0].reshape(groups * rows, -1)
    up_local = piece[1].reshape(groups * rows, -1)
    down_rows = down.shape[0] // groups
    qkv_block = lax.all_gather(qkv_local, "dp", axis=0, tiled=True)
    rest = [up_local, piece[2], piece[3]]
    flat = jnp.concatenate([r.reshape(-1) for r in rest])
    all_flat = lax.all_gather(flat, "dp", axis=0, tiled=False)
    dp_size = all_flat.shape[0]
    offs = [0, up_local.size, up_local.size + piece[2].size, flat.shape[0]]
    up_block = all_flat[:, offs[0]:offs[1]].reshape(dp_size * up_local.shape[0], -1)
    down_block = all_flat[:, offs[1]:offs[2]].reshape(dp_size, groups, down_rows, -1)
    out_full = all_flat[:, offs[2]:offs[3]].reshape(dp_size, groups, out.shape[0], -1)
    return qkv_block, up_block, down_block, out_full


def sum_scatter(part):
    groups = lax.axis_size("tensor")
    pieces = lax.all_to_all(part.reshape(groups, -1, part.shape[1]), "tensor", 0, 0, tiled=True)
    return jnp.sum(pieces.astype(jnp.float32), axis=0)


def gather_rows(rows):
    groups = lax.axis_size("tensor")
    spread = jnp.broadcast_to(rows[None], (groups,) + rows.shape)
    return lax.all_to_all(spread, "tensor", 0, 0, tiled=True).reshape(-1, rows.shape[1])


HEAD = D // H
INTERPRET = False
CHUNK = 4


def attention_kernel(list_ref, count_ref, q_ref, qid_ref, kt_ref, v_ref, kid_ref, o_ref, m_ref, l_ref, acc_ref):
    i = pl.program_id(0)
    pages = kt_ref.shape[0]
    page = kt_ref.shape[2]
    heads = q_ref.shape[1] // HEAD
    scale = 1.0 / math.sqrt(HEAD)
    q = q_ref[...]
    lane_head = lax.broadcasted_iota(jnp.int32, q.shape, 1) // HEAD
    head_q = [jnp.where(lane_head == h, q, jnp.zeros_like(q)) for h in range(heads)]
    qid = qid_ref[...]
    count = count_ref[i]
    m_ref[...] = jnp.full(m_ref.shape, -1e30, jnp.float32)
    l_ref[...] = jnp.zeros(l_ref.shape, jnp.float32)
    acc_ref[...] = jnp.zeros(acc_ref.shape, jnp.float32)
    slot_chunk = lax.broadcasted_iota(jnp.int32, (1, CHUNK * page), 1) // page

    def body(c, carry):
        base = c * CHUNK
        kps = [list_ref[i * (pages + CHUNK) + base + j] for j in range(CHUNK)]
        kt = jnp.concatenate([kt_ref[kp] for kp in kps], axis=1)
        v = jnp.concatenate([v_ref[kp] for kp in kps], axis=0)
        kid = jnp.concatenate([kid_ref[kp] for kp in kps], axis=1)
        allowed = jnp.logical_and(qid == kid, slot_chunk + base < count)
        for h in range(heads):
            s = jnp.dot(head_q[h], kt, preferred_element_type=jnp.float32) * scale
            s = jnp.where(allowed, s, -1e30)
            m_old = m_ref[h]
            m_new = jnp.maximum(m_old, jnp.max(s, axis=1, keepdims=True))
            p = jnp.where(allowed, jnp.exp(s - m_new), 0.0)
            alpha = jnp.exp(m_old - m_new)
            l_ref[h] = alpha * l_ref[h] + jnp.sum(p, axis=1, keepdims=True)
            acc_ref[h] = alpha * acc_ref[h] + jnp.dot(
                p.astype(jnp.bfloat16), v, preferred_element_type=jnp.float32
            )
            m_ref[h] = m_new
        return carry

    lax.fori_loop(0, (count + CHUNK - 1) // CHUNK, body, 0)
    out = acc_ref[0] / l_ref[0]
    for h in range(1, heads):
        out = jnp.where(lane_head == h, acc_ref[h] / l_ref[h], out)
    o_ref[...] = out.astype(o_ref.dtype)


def paged_attention(queries, keys, values, slot_request, dp_rank):
    pages, page = slot_request.shape
    rows, width = queries.shape
    own_pages = rows // page
    heads = width // HEAD
    present = (
        slot_request[:, :, None] == jnp.arange(-1, 4, dtype=jnp.int32)[None, None, :]
    ).any(axis=1).astype(jnp.float32)
    own = lax.dynamic_slice_in_dim(present, dp_rank * own_pages, own_pages, 0)
    allowed = (jnp.dot(own, present.T) > 0).astype(jnp.int32)
    counts = jnp.sum(allowed, axis=1)
    visit = jnp.argsort(1 - allowed, axis=1, stable=True).astype(jnp.int32)
    visit = jnp.pad(visit, ((0, 0), (0, CHUNK)), mode="edge").reshape(-1)
    own_ids = lax.dynamic_slice_in_dim(slot_request, dp_rank * own_pages, own_pages, 0)
    qid = own_ids.reshape(rows, 1)
    kid = slot_request.reshape(pages, 1, page)
    kt3 = jnp.transpose(keys.reshape(pages, page, width), (0, 2, 1))
    v3 = values.reshape(pages, page, width)
    grid_spec = pltpu.PrefetchScalarGridSpec(
        num_scalar_prefetch=2,
        grid=(own_pages,),
        in_specs=[
            pl.BlockSpec((page, width), lambda i, a, n: (i, 0)),
            pl.BlockSpec((page, 1), lambda i, a, n: (i, 0)),
            pl.BlockSpec((pages, width, page), lambda i, a, n: (0, 0, 0)),
            pl.BlockSpec((pages, page, width), lambda i, a, n: (0, 0, 0)),
            pl.BlockSpec((pages, 1, page), lambda i, a, n: (0, 0, 0)),
        ],
        out_specs=pl.BlockSpec((page, width), lambda i, a, n: (i, 0)),
        scratch_shapes=[
            pltpu.VMEM((heads, page, 1), jnp.float32),
            pltpu.VMEM((heads, page, 1), jnp.float32),
            pltpu.VMEM((heads, page, width), jnp.float32),
        ],
    )
    return pl.pallas_call(
        attention_kernel,
        grid_spec=grid_spec,
        out_shape=jax.ShapeDtypeStruct((rows, width), jnp.bfloat16),
        interpret=INTERPRET,
    )(visit, counts, queries, qid, kt3, v3, kid)


def shards(tokens, w_qkv, w_out, w_up, w_down, slot_request):
    groups = lax.axis_size("tensor")
    tensor_rank = lax.axis_index("tensor")
    qkv_block, up_block, down_block, out_full = spread_weights(w_qkv, w_out, w_up, w_down)
    tok_rows = tokens.shape[0]
    piece_rows = tok_rows // groups
    head_size = D // H
    heads_here = qkv_block.shape[1] // (3 * head_size)
    qkv = jnp.dot(tokens, qkv_block, preferred_element_type=jnp.float32).astype(jnp.bfloat16)
    qkv = qkv.reshape(tok_rows, heads_here, 3, head_size)
    queries = qkv[:, :, 0, :]
    key_rows = qkv[:, :, 1, :].reshape(tok_rows, heads_here * head_size)
    value_rows = qkv[:, :, 2, :].reshape(tok_rows, heads_here * head_size)
    slot_ids = slot_request.reshape(-1)
    own_ids = lax.dynamic_slice_in_dim(slot_ids, lax.axis_index("dp") * tok_rows, tok_rows, 0)

    kv_rows = jnp.concatenate([key_rows, value_rows], axis=1)
    kv_piece = lax.all_gather(kv_rows, "dp", axis=0, tiled=True)
    kv_piece, up_block, down_block, out_full = lax.optimization_barrier(
        (kv_piece, up_block, down_block, out_full)
    )
    kv_width = key_rows.shape[1]
    key_piece = kv_piece[:, :kv_width]
    value_piece = kv_piece[:, kv_width:]
    attn = paged_attention(
        queries.reshape(tok_rows, heads_here * head_size),
        key_piece,
        value_piece,
        slot_request,
        lax.axis_index("dp"),
    )
    my_ids = lax.dynamic_slice_in_dim(own_ids, tensor_rank * piece_rows, piece_rows, 0)
    spread = jnp.broadcast_to(attn[None], (groups,) + attn.shape)
    heads_all = lax.all_to_all(spread, "tensor", 0, 0, tiled=True)
    out_split = out_full.reshape(out_full.shape[0], groups, groups, -1, out_full.shape[3])
    proj = jnp.einsum(
        "tri,dstij->rdsj", heads_all, out_split, preferred_element_type=jnp.float32
    ).reshape(tok_rows, -1)
    first = layer_norm(tokens.astype(jnp.float32) + proj).astype(jnp.bfloat16)
    inner = jax.nn.gelu(
        jnp.dot(first, up_block, preferred_element_type=jnp.float32), approximate=False
    ).astype(jnp.bfloat16)
    partial = jnp.einsum("rk,dtkj->rdtj", inner, down_block, preferred_element_type=jnp.float32)
    ffn = sum_scatter(partial.reshape(tok_rows, -1).astype(jnp.bfloat16))
    first_rows = lax.dynamic_slice_in_dim(first, tensor_rank * piece_rows, piece_rows, 0)
    live = (my_ids >= 0).astype(jnp.float32)[:, None]
    encoded_rows = (layer_norm(first_rows.astype(jnp.float32) + ffn) * live).astype(jnp.bfloat16)
    return gather_rows(encoded_rows)


def solution(mesh):
    in_specs = (
        P("dp", None),
        P(("dp", "tensor"), None),
        P(None, ("dp", "tensor")),
        P(("dp", "tensor"), None),
        P(None, ("dp", "tensor")),
        P(),
    )
    out_specs = P("dp", None)
    return jax.shard_map(shards, mesh=mesh, in_specs=in_specs, out_specs=out_specs, check_vma=False)
```

```python
import math

import jax
import jax.numpy as jnp
from jax import lax
from jax.experimental import pallas as pl
from jax.experimental.pallas import tpu as pltpu
from jax.sharding import PartitionSpec as P

D = 1024
H = 16


def layer_norm(value):
    mean = jnp.mean(value, axis=-1, keepdims=True)
    centred = value - mean
    spread = jnp.mean(centred * centred, axis=-1, keepdims=True)
    return centred * lax.rsqrt(spread + 1e-05)


def spread_weights(w_qkv, w_out, w_up, w_down):
    groups = lax.axis_size("tensor")
    qkv = w_qkv.astype(jnp.bfloat16)
    up = w_up.astype(jnp.bfloat16)
    out_t = w_out.astype(jnp.bfloat16).T
    down_t = w_down.astype(jnp.bfloat16).T
    rows = qkv.shape[0]
    cols = out_t.shape[0]
    parts = [
        qkv.reshape(rows, groups, -1).transpose(1, 0, 2).reshape(groups, -1),
        up.reshape(rows, groups, -1).transpose(1, 0, 2).reshape(groups, -1),
        down_t.reshape(cols, groups, -1).transpose(1, 0, 2).reshape(groups, -1),
        jnp.broadcast_to(out_t.reshape(1, -1), (groups, out_t.size)),
    ]
    sizes = [p.shape[1] for p in parts]
    got = lax.all_to_all(jnp.concatenate(parts, axis=1), "tensor", 0, 0, tiled=True)
    cut = [sum(sizes[:k]) for k in range(5)]
    piece = [got[:, cut[k]:cut[k + 1]] for k in range(4)]
    qkv_local = piece[0].reshape(groups * rows, -1)
    width = up.shape[1] // groups
    up_local = piece[1].reshape(groups * rows, width)
    down_local = piece[2].reshape(-1, width)
    out_local = piece[3].reshape(-1, width)
    qkv_block = lax.all_gather(qkv_local, "dp", axis=0, tiled=True)
    rest = jnp.concatenate([up_local, down_local, out_local], axis=0)
    all_rest = lax.all_gather(rest, "dp", axis=0, tiled=False)
    dp_size = all_rest.shape[0]
    offs = [0, up_local.shape[0], up_local.shape[0] + down_local.shape[0], rest.shape[0]]
    up_block = all_rest[:, offs[0]:offs[1]].reshape(dp_size * up_local.shape[0], width)
    down_full = all_rest[:, offs[1]:offs[2]].reshape(dp_size, groups, cols, -1)
    out_full = all_rest[:, offs[2]:offs[3]].reshape(dp_size, groups, cols, -1)
    return qkv_block, up_block, down_full, out_full


def sum_scatter(part):
    groups = lax.axis_size("tensor")
    pieces = lax.all_to_all(part.reshape(groups, -1, part.shape[1]), "tensor", 0, 0, tiled=True)
    return jnp.sum(pieces.astype(jnp.float32), axis=0)


def gather_rows(rows):
    groups = lax.axis_size("tensor")
    spread = jnp.broadcast_to(rows[None], (groups,) + rows.shape)
    return lax.all_to_all(spread, "tensor", 0, 0, tiled=True).reshape(-1, rows.shape[1])


HEAD = D // H
INTERPRET = False
CHUNK = 4


def attention_kernel(list_ref, count_ref, q_ref, qid_ref, kv_ref, kid_ref, o_ref, m_ref, l_ref, acc_ref):
    i = pl.program_id(0)
    pages = kv_ref.shape[0]
    page = kv_ref.shape[1]
    width = q_ref.shape[1]
    heads = width // HEAD
    scale = 1.0 / math.sqrt(HEAD)
    q = q_ref[...]
    lane_head = lax.broadcasted_iota(jnp.int32, q.shape, 1) // HEAD
    head_q = [jnp.where(lane_head == h, q, jnp.zeros_like(q)) for h in range(heads)]
    qid = qid_ref[...]
    count = count_ref[i]
    m_ref[...] = jnp.full(m_ref.shape, -1e30, jnp.float32)
    l_ref[...] = jnp.zeros(l_ref.shape, jnp.float32)
    acc_ref[...] = jnp.zeros(acc_ref.shape, jnp.float32)
    slot_chunk = lax.broadcasted_iota(jnp.int32, (1, CHUNK * page), 1) // page

    def body(c, carry):
        base = c * CHUNK
        kps = [list_ref[i * (pages + CHUNK) + base + j] for j in range(CHUNK)]
        kv = jnp.concatenate([kv_ref[kp] for kp in kps], axis=0)
        k = kv[:, :width]
        v = kv[:, width:]
        kid = jnp.concatenate([kid_ref[kp] for kp in kps], axis=1)
        allowed = jnp.logical_and(qid == kid, slot_chunk + base < count)
        for h in range(heads):
            s = lax.dot_general(
                head_q[h], k, (((1,), (1,)), ((), ())), preferred_element_type=jnp.float32
            ) * scale
            s = jnp.where(allowed, s, -1e30)
            m_old = m_ref[h]
            m_new = jnp.maximum(m_old, jnp.max(s, axis=1, keepdims=True))
            p = jnp.where(allowed, jnp.exp(s - m_new), 0.0)
            alpha = jnp.exp(m_old - m_new)
            l_ref[h] = alpha * l_ref[h] + jnp.sum(p, axis=1, keepdims=True)
            acc_ref[h] = alpha * acc_ref[h] + jnp.dot(
                p.astype(jnp.bfloat16), v, preferred_element_type=jnp.float32
            )
            m_ref[h] = m_new
        return carry

    lax.fori_loop(0, (count + CHUNK - 1) // CHUNK, body, 0)
    out = acc_ref[0] / l_ref[0]
    for h in range(1, heads):
        out = jnp.where(lane_head == h, acc_ref[h] / l_ref[h], out)
    o_ref[...] = out.astype(o_ref.dtype)


def paged_attention(queries, kv, slot_request, dp_rank):
    pages, page = slot_request.shape
    rows, width = queries.shape
    own_pages = rows // page
    heads = width // HEAD
    present = (
        slot_request[:, :, None] == jnp.arange(-1, 4, dtype=jnp.int32)[None, None, :]
    ).any(axis=1).astype(jnp.float32)
    own = lax.dynamic_slice_in_dim(present, dp_rank * own_pages, own_pages, 0)
    allowed = (jnp.dot(own, present.T) > 0).astype(jnp.int32)
    counts = jnp.sum(allowed, axis=1)
    visit = jnp.argsort(1 - allowed, axis=1, stable=True).astype(jnp.int32)
    visit = jnp.pad(visit, ((0, 0), (0, CHUNK)), mode="edge").reshape(-1)
    own_ids = lax.dynamic_slice_in_dim(slot_request, dp_rank * own_pages, own_pages, 0)
    qid = own_ids.reshape(rows, 1)
    kid = slot_request.reshape(pages, 1, page)
    kv3 = kv.reshape(pages, page, 2 * width)
    grid_spec = pltpu.PrefetchScalarGridSpec(
        num_scalar_prefetch=2,
        grid=(own_pages,),
        in_specs=[
            pl.BlockSpec((page, width), lambda i, a, n: (i, 0)),
            pl.BlockSpec((page, 1), lambda i, a, n: (i, 0)),
            pl.BlockSpec((pages, page, 2 * width), lambda i, a, n: (0, 0, 0)),
            pl.BlockSpec((pages, 1, page), lambda i, a, n: (0, 0, 0)),
        ],
        out_specs=pl.BlockSpec((page, width), lambda i, a, n: (i, 0)),
        scratch_shapes=[
            pltpu.VMEM((heads, page, 1), jnp.float32),
            pltpu.VMEM((heads, page, 1), jnp.float32),
            pltpu.VMEM((heads, page, width), jnp.float32),
        ],
    )
    return pl.pallas_call(
        attention_kernel,
        grid_spec=grid_spec,
        out_shape=jax.ShapeDtypeStruct((rows, width), jnp.bfloat16),
        interpret=INTERPRET,
    )(visit, counts, queries, qid, kv3, kid)


def shards(tokens, w_qkv, w_out, w_up, w_down, slot_request):
    groups = lax.axis_size("tensor")
    tensor_rank = lax.axis_index("tensor")
    qkv_block, up_block, down_block, out_full = spread_weights(w_qkv, w_out, w_up, w_down)
    tok_rows = tokens.shape[0]
    piece_rows = tok_rows // groups
    head_size = D // H
    heads_here = qkv_block.shape[1] // (3 * head_size)
    qkv = jnp.dot(tokens, qkv_block, preferred_element_type=jnp.float32).astype(jnp.bfloat16)
    qkv = qkv.reshape(tok_rows, heads_here, 3, head_size)
    queries = qkv[:, :, 0, :]
    key_rows = qkv[:, :, 1, :].reshape(tok_rows, heads_here * head_size)
    value_rows = qkv[:, :, 2, :].reshape(tok_rows, heads_here * head_size)
    slot_ids = slot_request.reshape(-1)
    own_ids = lax.dynamic_slice_in_dim(slot_ids, lax.axis_index("dp") * tok_rows, tok_rows, 0)

    kv_rows = jnp.concatenate([key_rows, value_rows], axis=1)
    kv_piece = lax.all_gather(kv_rows, "dp", axis=0, tiled=False)
    kv_piece, up_block, down_block, out_full = lax.optimization_barrier(
        (kv_piece, up_block, down_block, out_full)
    )
    attn = paged_attention(
        queries.reshape(tok_rows, heads_here * head_size),
        kv_piece,
        slot_request,
        lax.axis_index("dp"),
    )
    my_ids = lax.dynamic_slice_in_dim(own_ids, tensor_rank * piece_rows, piece_rows, 0)
    spread = jnp.broadcast_to(attn[None], (groups,) + attn.shape)
    heads_all = lax.all_to_all(spread, "tensor", 0, 2, tiled=True).reshape(tok_rows, -1)
    out_cols = out_full.reshape(-1, out_full.shape[3])
    proj = lax.dot_general(
        heads_all, out_cols, (((1,), (1,)), ((), ())), preferred_element_type=jnp.float32
    )
    first = layer_norm(tokens.astype(jnp.float32) + proj).astype(jnp.bfloat16)
    inner = jax.nn.gelu(
        jnp.dot(first, up_block, preferred_element_type=jnp.float32), approximate=False
    ).astype(jnp.bfloat16)
    down_cols = down_block.reshape(-1, down_block.shape[3])
    partial = lax.dot_general(
        inner, down_cols, (((1,), (1,)), ((), ())), preferred_element_type=jnp.float32
    )
    ffn = sum_scatter(partial.astype(jnp.bfloat16))
    first_rows = lax.dynamic_slice_in_dim(first, tensor_rank * piece_rows, piece_rows, 0)
    live = (my_ids >= 0).astype(jnp.float32)[:, None]
    encoded_rows = (layer_norm(first_rows.astype(jnp.float32) + ffn) * live).astype(jnp.bfloat16)
    return gather_rows(encoded_rows)


def solution(mesh):
    in_specs = (
        P("dp", None),
        P(("dp", "tensor"), None),
        P(None, ("dp", "tensor")),
        P(("dp", "tensor"), None),
        P(None, ("dp", "tensor")),
        P(),
    )
    out_specs = P("dp", None)
    return jax.shard_map(shards, mesh=mesh, in_specs=in_specs, out_specs=out_specs, check_vma=False)
```

```python
import math

import jax
import jax.numpy as jnp
from jax import lax
from jax.experimental import pallas as pl
from jax.experimental.pallas import tpu as pltpu
from jax.sharding import PartitionSpec as P

D = 1024
H = 16


def layer_norm(value):
    mean = jnp.mean(value, axis=-1, keepdims=True)
    centred = value - mean
    spread = jnp.mean(centred * centred, axis=-1, keepdims=True)
    return centred * lax.rsqrt(spread + 1e-05)


def spread_weights(w_qkv, w_out, w_up, w_down):
    groups = lax.axis_size("tensor")
    qkv = w_qkv.astype(jnp.bfloat16)
    up = w_up.astype(jnp.bfloat16)
    out_t = w_out.astype(jnp.bfloat16).T
    down_t = w_down.astype(jnp.bfloat16).T
    rows = qkv.shape[0]
    cols = out_t.shape[0]
    parts = [
        qkv.reshape(rows, groups, -1).transpose(1, 0, 2).reshape(groups, -1),
        up.reshape(rows, groups, -1).transpose(1, 0, 2).reshape(groups, -1),
        down_t.reshape(cols, groups, -1).transpose(1, 0, 2).reshape(groups, -1),
        jnp.broadcast_to(out_t.reshape(1, -1), (groups, out_t.size)),
    ]
    sizes = [p.shape[1] for p in parts]
    got = lax.all_to_all(jnp.concatenate(parts, axis=1), "tensor", 0, 0, tiled=True)
    cut = [sum(sizes[:k]) for k in range(5)]
    piece = [got[:, cut[k]:cut[k + 1]] for k in range(4)]
    qkv_local = piece[0].reshape(groups * rows, -1)
    width = up.shape[1] // groups
    up_local = piece[1].reshape(groups * rows, width)
    down_local = piece[2].reshape(-1, width)
    out_local = piece[3].reshape(-1, width)
    qkv_block = lax.all_gather(qkv_local, "dp", axis=0, tiled=True)
    rest = jnp.concatenate([up_local, down_local, out_local], axis=0)
    all_rest = lax.all_gather(rest, "dp", axis=0, tiled=False)
    dp_size = all_rest.shape[0]
    offs = [0, up_local.shape[0], up_local.shape[0] + down_local.shape[0], rest.shape[0]]
    up_block = all_rest[:, offs[0]:offs[1]].reshape(dp_size * up_local.shape[0], width)
    down_full = all_rest[:, offs[1]:offs[2]].reshape(dp_size, groups, cols, -1)
    out_full = all_rest[:, offs[2]:offs[3]].reshape(dp_size, groups, cols, -1)
    return qkv_block, up_block, down_full, out_full


def sum_scatter(part):
    groups = lax.axis_size("tensor")
    pieces = lax.all_to_all(part.reshape(groups, -1, part.shape[1]), "tensor", 0, 0, tiled=True)
    return jnp.sum(pieces.astype(jnp.float32), axis=0)


def gather_rows(rows):
    groups = lax.axis_size("tensor")
    spread = jnp.broadcast_to(rows[None], (groups,) + rows.shape)
    return lax.all_to_all(spread, "tensor", 0, 0, tiled=True).reshape(-1, rows.shape[1])


HEAD = D // H
INTERPRET = False
CHUNK = 16


def attention_kernel(list_ref, count_ref, q_ref, qid_ref, kv_ref, kid_ref, o_ref, m_ref, l_ref, acc_ref):
    i = pl.program_id(0)
    pages = kv_ref.shape[0]
    page = kv_ref.shape[1]
    width = q_ref.shape[1]
    heads = width // HEAD
    scale = 1.0 / math.sqrt(HEAD)
    q = q_ref[...]
    lane_head = lax.broadcasted_iota(jnp.int32, q.shape, 1) // HEAD
    head_q = [jnp.where(lane_head == h, q, jnp.zeros_like(q)) for h in range(heads)]
    qid = qid_ref[...]
    count = count_ref[i]
    m_ref[...] = jnp.full(m_ref.shape, -1e30, jnp.float32)
    l_ref[...] = jnp.zeros(l_ref.shape, jnp.float32)
    acc_ref[...] = jnp.zeros(acc_ref.shape, jnp.float32)
    slot_chunk = lax.broadcasted_iota(jnp.int32, (1, CHUNK * page), 1) // page

    def body(c, carry):
        base = c * CHUNK
        kps = [list_ref[i * (pages + CHUNK) + base + j] for j in range(CHUNK)]
        kv = jnp.concatenate([kv_ref[kp] for kp in kps], axis=0)
        k = kv[:, :width]
        v = kv[:, width:]
        kid = jnp.concatenate([kid_ref[kp] for kp in kps], axis=1)
        allowed = jnp.logical_and(qid == kid, slot_chunk + base < count)
        for h in range(heads):
            s = lax.dot_general(
                head_q[h], k, (((1,), (1,)), ((), ())), preferred_element_type=jnp.float32
            )
            s = jnp.where(allowed, s * scale, -jnp.inf)
            m_old = m_ref[h]
            m_new = jnp.maximum(m_old, jnp.max(s, axis=1, keepdims=True))
            p = jnp.exp(s - m_new)
            alpha = jnp.exp(m_old - m_new)
            l_ref[h] = alpha * l_ref[h] + jnp.sum(p, axis=1, keepdims=True)
            acc_ref[h] = alpha * acc_ref[h] + jnp.dot(
                p.astype(jnp.bfloat16), v, preferred_element_type=jnp.float32
            )
            m_ref[h] = m_new
        return carry

    lax.fori_loop(0, (count + CHUNK - 1) // CHUNK, body, 0)
    out = acc_ref[0] / l_ref[0]
    for h in range(1, heads):
        out = jnp.where(lane_head == h, acc_ref[h] / l_ref[h], out)
    o_ref[...] = out.astype(o_ref.dtype)


def paged_attention(queries, kv, slot_request, dp_rank):
    pages, page = slot_request.shape
    rows, width = queries.shape
    own_pages = rows // page
    heads = width // HEAD
    present = (
        slot_request[:, :, None] == jnp.arange(-1, 4, dtype=jnp.int32)[None, None, :]
    ).any(axis=1).astype(jnp.float32)
    own = lax.dynamic_slice_in_dim(present, dp_rank * own_pages, own_pages, 0)
    allowed = (jnp.dot(own, present.T) > 0).astype(jnp.int32)
    counts = jnp.sum(allowed, axis=1)
    visit = jnp.argsort(1 - allowed, axis=1, stable=True).astype(jnp.int32)
    visit = jnp.pad(visit, ((0, 0), (0, CHUNK)), mode="edge").reshape(-1)
    own_ids = lax.dynamic_slice_in_dim(slot_request, dp_rank * own_pages, own_pages, 0)
    qid = own_ids.reshape(rows, 1)
    kid = slot_request.reshape(pages, 1, page)
    kv3 = kv.reshape(pages, page, 2 * width)
    grid_spec = pltpu.PrefetchScalarGridSpec(
        num_scalar_prefetch=2,
        grid=(own_pages,),
        in_specs=[
            pl.BlockSpec((page, width), lambda i, a, n: (i, 0)),
            pl.BlockSpec((page, 1), lambda i, a, n: (i, 0)),
            pl.BlockSpec((pages, page, 2 * width), lambda i, a, n: (0, 0, 0)),
            pl.BlockSpec((pages, 1, page), lambda i, a, n: (0, 0, 0)),
        ],
        out_specs=pl.BlockSpec((page, width), lambda i, a, n: (i, 0)),
        scratch_shapes=[
            pltpu.VMEM((heads, page, 1), jnp.float32),
            pltpu.VMEM((heads, page, 1), jnp.float32),
            pltpu.VMEM((heads, page, width), jnp.float32),
        ],
    )
    return pl.pallas_call(
        attention_kernel,
        grid_spec=grid_spec,
        out_shape=jax.ShapeDtypeStruct((rows, width), jnp.bfloat16),
        interpret=INTERPRET,
    )(visit, counts, queries, qid, kv3, kid)


def shards(tokens, w_qkv, w_out, w_up, w_down, slot_request):
    groups = lax.axis_size("tensor")
    tensor_rank = lax.axis_index("tensor")
    qkv_block, up_block, down_block, out_full = spread_weights(w_qkv, w_out, w_up, w_down)
    tok_rows = tokens.shape[0]
    piece_rows = tok_rows // groups
    head_size = D // H
    heads_here = qkv_block.shape[1] // (3 * head_size)
    qkv = jnp.dot(tokens, qkv_block, preferred_element_type=jnp.float32).astype(jnp.bfloat16)
    qkv = qkv.reshape(tok_rows, heads_here, 3, head_size)
    queries = qkv[:, :, 0, :]
    key_rows = qkv[:, :, 1, :].reshape(tok_rows, heads_here * head_size)
    value_rows = qkv[:, :, 2, :].reshape(tok_rows, heads_here * head_size)
    slot_ids = slot_request.reshape(-1)
    own_ids = lax.dynamic_slice_in_dim(slot_ids, lax.axis_index("dp") * tok_rows, tok_rows, 0)

    kv_rows = jnp.concatenate([key_rows, value_rows], axis=1)
    kv_piece = lax.all_gather(kv_rows, "dp", axis=0, tiled=False)
    kv_piece, up_block, down_block, out_full = lax.optimization_barrier(
        (kv_piece, up_block, down_block, out_full)
    )
    attn = paged_attention(
        queries.reshape(tok_rows, heads_here * head_size),
        kv_piece,
        slot_request,
        lax.axis_index("dp"),
    )
    my_ids = lax.dynamic_slice_in_dim(own_ids, tensor_rank * piece_rows, piece_rows, 0)
    spread = jnp.broadcast_to(attn[None], (groups,) + attn.shape)
    heads_all = lax.all_to_all(spread, "tensor", 0, 2, tiled=True).reshape(tok_rows, -1)
    out_cols = out_full.reshape(-1, out_full.shape[3])
    proj = lax.dot_general(
        heads_all, out_cols, (((1,), (1,)), ((), ())), preferred_element_type=jnp.float32
    )
    first = layer_norm(tokens.astype(jnp.float32) + proj).astype(jnp.bfloat16)
    inner = jax.nn.gelu(
        jnp.dot(first, up_block, preferred_element_type=jnp.float32), approximate=False
    ).astype(jnp.bfloat16)
    down_cols = down_block.reshape(-1, down_block.shape[3])
    partial = lax.dot_general(
        inner, down_cols, (((1,), (1,)), ((), ())), preferred_element_type=jnp.float32
    )
    ffn = sum_scatter(partial.astype(jnp.bfloat16))
    first_rows = lax.dynamic_slice_in_dim(first, tensor_rank * piece_rows, piece_rows, 0)
    live = (my_ids >= 0).astype(jnp.float32)[:, None]
    encoded_rows = (layer_norm(first_rows.astype(jnp.float32) + ffn) * live).astype(jnp.bfloat16)
    return gather_rows(encoded_rows)


def solution(mesh):
    in_specs = (
        P("dp", None),
        P(("dp", "tensor"), None),
        P(None, ("dp", "tensor")),
        P(("dp", "tensor"), None),
        P(None, ("dp", "tensor")),
        P(),
    )
    out_specs = P("dp", None)
    return jax.shard_map(shards, mesh=mesh, in_specs=in_specs, out_specs=out_specs, check_vma=False)
```

```python
import math

import jax
import jax.numpy as jnp
from jax import lax
from jax.experimental import pallas as pl
from jax.experimental.pallas import tpu as pltpu
from jax.sharding import PartitionSpec as P

D = 1024
H = 16


def layer_norm(value):
    mean = jnp.mean(value, axis=-1, keepdims=True)
    centred = value - mean
    spread = jnp.mean(centred * centred, axis=-1, keepdims=True)
    return centred * lax.rsqrt(spread + 1e-05)


def spread_weights(w_qkv, w_out, w_up, w_down):
    groups = lax.axis_size("tensor")
    qkv = w_qkv.astype(jnp.bfloat16)
    up = w_up.astype(jnp.bfloat16)
    out_t = w_out.astype(jnp.bfloat16).T
    down_t = w_down.astype(jnp.bfloat16).T
    rows = qkv.shape[0]
    cols = out_t.shape[0]
    parts = [
        qkv.reshape(rows, groups, -1).transpose(1, 0, 2).reshape(groups, -1),
        up.reshape(rows, groups, -1).transpose(1, 0, 2).reshape(groups, -1),
        down_t.reshape(cols, groups, -1).transpose(1, 0, 2).reshape(groups, -1),
        jnp.broadcast_to(out_t.reshape(1, -1), (groups, out_t.size)),
    ]
    sizes = [p.shape[1] for p in parts]
    got = lax.all_to_all(jnp.concatenate(parts, axis=1), "tensor", 0, 0, tiled=True)
    cut = [sum(sizes[:k]) for k in range(5)]
    piece = [got[:, cut[k]:cut[k + 1]] for k in range(4)]
    qkv_local = piece[0].reshape(groups * rows, -1)
    width = up.shape[1] // groups
    up_local = piece[1].reshape(groups * rows, width)
    down_local = piece[2].reshape(-1, width)
    out_local = piece[3].reshape(-1, width)
    qkv_block = lax.all_gather(qkv_local, "dp", axis=0, tiled=True)
    rest = jnp.concatenate([up_local, down_local, out_local], axis=0)
    all_rest = lax.all_gather(rest, "dp", axis=0, tiled=False)
    dp_size = all_rest.shape[0]
    offs = [0, up_local.shape[0], up_local.shape[0] + down_local.shape[0], rest.shape[0]]
    up_block = all_rest[:, offs[0]:offs[1]].reshape(dp_size * up_local.shape[0], width)
    down_full = all_rest[:, offs[1]:offs[2]].reshape(dp_size, groups, cols, -1)
    out_full = all_rest[:, offs[2]:offs[3]].reshape(dp_size, groups, cols, -1)
    return qkv_block, up_block, down_full, out_full


def sum_scatter(part):
    groups = lax.axis_size("tensor")
    pieces = lax.all_to_all(part.reshape(groups, -1, part.shape[1]), "tensor", 0, 0, tiled=True)
    return jnp.sum(pieces.astype(jnp.float32), axis=0)


def gather_rows(rows):
    groups = lax.axis_size("tensor")
    spread = jnp.broadcast_to(rows[None], (groups,) + rows.shape)
    return lax.all_to_all(spread, "tensor", 0, 0, tiled=True).reshape(-1, rows.shape[1])


HEAD = D // H
INTERPRET = False
CHUNK = 16


def attention_kernel(list_ref, count_ref, q_ref, qid_ref, kv_ref, kid_ref, o_ref, m_ref, l_ref, acc_ref):
    i = pl.program_id(0)
    pages = kv_ref.shape[0]
    page = kv_ref.shape[1]
    width = q_ref.shape[1]
    heads = width // HEAD
    scale = 1.0 / math.sqrt(HEAD)
    q = q_ref[...]
    lane_head = lax.broadcasted_iota(jnp.int32, q.shape, 1) // HEAD
    head_q = [jnp.where(lane_head == h, q, jnp.zeros_like(q)) for h in range(heads)]
    qid = qid_ref[...]
    count = count_ref[i]
    m_ref[...] = jnp.full(m_ref.shape, -1e30, jnp.float32)
    l_ref[...] = jnp.zeros(l_ref.shape, jnp.float32)
    acc_ref[...] = jnp.zeros(acc_ref.shape, jnp.float32)
    slot_chunk = lax.broadcasted_iota(jnp.int32, (1, CHUNK * page), 1) // page

    def body(c, carry):
        base = c * CHUNK
        kps = [list_ref[i * (pages + CHUNK) + base + j] for j in range(CHUNK)]
        kv = jnp.concatenate([kv_ref[kp] for kp in kps], axis=0)
        k = kv[:, :width]
        v = kv[:, width:]
        kid = jnp.concatenate([kid_ref[kp] for kp in kps], axis=1)
        allowed = jnp.logical_and(qid == kid, slot_chunk + base < count)
        for h in range(heads):
            s = lax.dot_general(
                head_q[h], k, (((1,), (1,)), ((), ())), preferred_element_type=jnp.float32
            )
            s = jnp.where(allowed, s * scale, -jnp.inf)
            m_old = m_ref[h]
            m_new = jnp.maximum(m_old, jnp.max(s, axis=1, keepdims=True))
            p = jnp.exp(s - m_new)
            alpha = jnp.exp(m_old - m_new)
            l_ref[h] = alpha * l_ref[h] + jnp.sum(p, axis=1, keepdims=True)
            acc_ref[h] = alpha * acc_ref[h] + jnp.dot(
                p.astype(jnp.bfloat16), v, preferred_element_type=jnp.float32
            )
            m_ref[h] = m_new
        return carry

    lax.fori_loop(0, (count + CHUNK - 1) // CHUNK, body, 0)
    out = acc_ref[0] / l_ref[0]
    for h in range(1, heads):
        out = jnp.where(lane_head == h, acc_ref[h] / l_ref[h], out)
    o_ref[...] = out.astype(o_ref.dtype)


def paged_attention(queries, kv, slot_request, first_page):
    pages, page = slot_request.shape
    rows, width = queries.shape
    own_pages = rows // page
    heads = width // HEAD
    present = (
        slot_request[:, :, None] == jnp.arange(-1, 4, dtype=jnp.int32)[None, None, :]
    ).any(axis=1).astype(jnp.float32)
    own = lax.dynamic_slice_in_dim(present, first_page, own_pages, 0)
    allowed = (jnp.dot(own, present.T) > 0).astype(jnp.int32)
    counts = jnp.sum(allowed, axis=1)
    visit = jnp.argsort(1 - allowed, axis=1, stable=True).astype(jnp.int32)
    visit = jnp.pad(visit, ((0, 0), (0, CHUNK)), mode="edge").reshape(-1)
    own_ids = lax.dynamic_slice_in_dim(slot_request, first_page, own_pages, 0)
    qid = own_ids.reshape(rows, 1)
    kid = slot_request.reshape(pages, 1, page)
    kv3 = kv.reshape(pages, page, 2 * width)
    grid_spec = pltpu.PrefetchScalarGridSpec(
        num_scalar_prefetch=2,
        grid=(own_pages,),
        in_specs=[
            pl.BlockSpec((page, width), lambda i, a, n: (i, 0)),
            pl.BlockSpec((page, 1), lambda i, a, n: (i, 0)),
            pl.BlockSpec((pages, page, 2 * width), lambda i, a, n: (0, 0, 0)),
            pl.BlockSpec((pages, 1, page), lambda i, a, n: (0, 0, 0)),
        ],
        out_specs=pl.BlockSpec((page, width), lambda i, a, n: (i, 0)),
        scratch_shapes=[
            pltpu.VMEM((heads, page, 1), jnp.float32),
            pltpu.VMEM((heads, page, 1), jnp.float32),
            pltpu.VMEM((heads, page, width), jnp.float32),
        ],
    )
    return pl.pallas_call(
        attention_kernel,
        grid_spec=grid_spec,
        out_shape=jax.ShapeDtypeStruct((rows, width), jnp.bfloat16),
        interpret=INTERPRET,
    )(visit, counts, queries, qid, kv3, kid)


def shards(tokens, w_qkv, w_out, w_up, w_down, slot_request):
    groups = lax.axis_size("tensor")
    tensor_rank = lax.axis_index("tensor")
    qkv_block, up_block, down_block, out_full = spread_weights(w_qkv, w_out, w_up, w_down)
    tok_rows = tokens.shape[0]
    piece_rows = tok_rows // groups
    head_size = D // H
    heads_here = qkv_block.shape[1] // (3 * head_size)
    qkv = jnp.dot(tokens, qkv_block, preferred_element_type=jnp.float32).astype(jnp.bfloat16)
    qkv = qkv.reshape(tok_rows, heads_here, 3, head_size)
    queries = qkv[:, :, 0, :]
    key_rows = qkv[:, :, 1, :].reshape(tok_rows, heads_here * head_size)
    value_rows = qkv[:, :, 2, :].reshape(tok_rows, heads_here * head_size)
    slot_ids = slot_request.reshape(-1)
    own_ids = lax.dynamic_slice_in_dim(slot_ids, lax.axis_index("dp") * tok_rows, tok_rows, 0)

    kv_rows = jnp.concatenate([key_rows, value_rows], axis=1)
    kv_piece = lax.all_gather(kv_rows, "dp", axis=0, tiled=False)
    kv_piece, up_block, down_block, out_full = lax.optimization_barrier(
        (kv_piece, up_block, down_block, out_full)
    )
    q_rows = queries.reshape(tok_rows, heads_here * head_size)
    page = slot_request.shape[1]
    halves = 2
    half_rows = tok_rows // halves
    slice_rows = half_rows // groups
    out_cols = out_full.reshape(-1, out_full.shape[3])
    down_cols = down_block.reshape(-1, down_block.shape[3])
    encoded = []
    for half in range(halves):
        lo = half * half_rows
        attn = paged_attention(
            q_rows[lo:lo + half_rows],
            kv_piece,
            slot_request,
            (lax.axis_index("dp") * tok_rows + lo) // page,
        )
        spread = jnp.broadcast_to(attn[None], (groups,) + attn.shape)
        heads_all = lax.all_to_all(spread, "tensor", 0, 2, tiled=True).reshape(half_rows, -1)
        proj = lax.dot_general(
            heads_all, out_cols, (((1,), (1,)), ((), ())), preferred_element_type=jnp.float32
        )
        first = layer_norm(tokens[lo:lo + half_rows].astype(jnp.float32) + proj).astype(jnp.bfloat16)
        inner = jax.nn.gelu(
            jnp.dot(first, up_block, preferred_element_type=jnp.float32), approximate=False
        ).astype(jnp.bfloat16)
        partial = lax.dot_general(
            inner, down_cols, (((1,), (1,)), ((), ())), preferred_element_type=jnp.float32
        )
        ffn = sum_scatter(partial.astype(jnp.bfloat16))
        first_rows = lax.dynamic_slice_in_dim(first, tensor_rank * slice_rows, slice_rows, 0)
        my_ids = lax.dynamic_slice_in_dim(own_ids, lo + tensor_rank * slice_rows, slice_rows, 0)
        live = (my_ids >= 0).astype(jnp.float32)[:, None]
        encoded_rows = (layer_norm(first_rows.astype(jnp.float32) + ffn) * live).astype(jnp.bfloat16)
        encoded.append(gather_rows(encoded_rows))
    return jnp.concatenate(encoded, axis=0)


def solution(mesh):
    in_specs = (
        P("dp", None),
        P(("dp", "tensor"), None),
        P(None, ("dp", "tensor")),
        P(("dp", "tensor"), None),
        P(None, ("dp", "tensor")),
        P(),
    )
    out_specs = P("dp", None)
    return jax.shard_map(shards, mesh=mesh, in_specs=in_specs, out_specs=out_specs, check_vma=False)
```

```python
import math

import jax
import jax.numpy as jnp
from jax import lax
from jax.experimental import pallas as pl
from jax.experimental.pallas import tpu as pltpu
from jax.sharding import PartitionSpec as P

D = 1024
H = 16


def layer_norm(value):
    mean = jnp.mean(value, axis=-1, keepdims=True)
    centred = value - mean
    spread = jnp.mean(centred * centred, axis=-1, keepdims=True)
    return centred * lax.rsqrt(spread + 1e-05)


def spread_weights(w_qkv, w_out, w_up, w_down):
    groups = lax.axis_size("tensor")
    qkv = w_qkv.astype(jnp.bfloat16)
    up = w_up.astype(jnp.bfloat16)
    out_t = w_out.astype(jnp.bfloat16).T
    down_t = w_down.astype(jnp.bfloat16).T
    rows = qkv.shape[0]
    cols = out_t.shape[0]
    dp_size = lax.axis_size("dp")
    qkv_parts = qkv.reshape(rows, groups, -1).transpose(1, 0, 2)
    qkv_send = jnp.broadcast_to(qkv_parts[None], (dp_size,) + qkv_parts.shape)
    qkv_got = lax.all_to_all(
        qkv_send.reshape((dp_size * groups,) + qkv_parts.shape[1:]), ("dp", "tensor"), 0, 0, tiled=True
    )
    qkv_block = qkv_got.reshape(-1, qkv_parts.shape[2])
    parts = [
        up.reshape(rows, groups, -1).transpose(1, 0, 2).reshape(groups, -1),
        down_t.reshape(cols, groups, -1).transpose(1, 0, 2).reshape(groups, -1),
        jnp.broadcast_to(out_t.reshape(1, -1), (groups, out_t.size)),
    ]
    sizes = [p.shape[1] for p in parts]
    got = lax.all_to_all(jnp.concatenate(parts, axis=1), "tensor", 0, 0, tiled=True)
    cut = [sum(sizes[:k]) for k in range(4)]
    piece = [got[:, cut[k]:cut[k + 1]] for k in range(3)]
    width = up.shape[1] // groups
    up_local = piece[0].reshape(groups * rows, width)
    down_local = piece[1].reshape(-1, width)
    out_local = piece[2].reshape(-1, width)
    rest = jnp.concatenate([up_local, down_local, out_local], axis=0)
    all_rest = lax.all_gather(rest, "dp", axis=0, tiled=False)
    dp_size = all_rest.shape[0]
    offs = [0, up_local.shape[0], up_local.shape[0] + down_local.shape[0], rest.shape[0]]
    up_block = all_rest[:, offs[0]:offs[1]].reshape(dp_size * up_local.shape[0], width)
    down_full = all_rest[:, offs[1]:offs[2]].reshape(dp_size, groups, cols, -1)
    out_full = all_rest[:, offs[2]:offs[3]].reshape(dp_size, groups, cols, -1)
    return qkv_block, up_block, down_full, out_full


def sum_scatter(part):
    groups = lax.axis_size("tensor")
    pieces = lax.all_to_all(part.reshape(groups, -1, part.shape[1]), "tensor", 0, 0, tiled=True)
    return jnp.sum(pieces.astype(jnp.float32), axis=0)


def gather_rows(rows):
    groups = lax.axis_size("tensor")
    spread = jnp.broadcast_to(rows[None], (groups,) + rows.shape)
    return lax.all_to_all(spread, "tensor", 0, 0, tiled=True).reshape(-1, rows.shape[1])


HEAD = D // H
INTERPRET = False
CHUNK = 16


def attention_kernel(list_ref, count_ref, q_ref, qid_ref, kv_ref, kid_ref, o_ref, m_ref, l_ref, acc_ref):
    i = pl.program_id(0)
    pages = kv_ref.shape[0]
    page = kv_ref.shape[1]
    width = q_ref.shape[1]
    heads = width // HEAD
    scale = 1.0 / math.sqrt(HEAD)
    q = q_ref[...]
    lane_head = lax.broadcasted_iota(jnp.int32, q.shape, 1) // HEAD
    head_q = [jnp.where(lane_head == h, q, jnp.zeros_like(q)) for h in range(heads)]
    qid = qid_ref[...]
    count = count_ref[i]
    m_ref[...] = jnp.full(m_ref.shape, -1e30, jnp.float32)
    l_ref[...] = jnp.zeros(l_ref.shape, jnp.float32)
    acc_ref[...] = jnp.zeros(acc_ref.shape, jnp.float32)
    slot_chunk = lax.broadcasted_iota(jnp.int32, (1, CHUNK * page), 1) // page

    def body(c, carry):
        base = c * CHUNK
        kps = [list_ref[i * (pages + CHUNK) + base + j] for j in range(CHUNK)]
        kv = jnp.concatenate([kv_ref[kp] for kp in kps], axis=0)
        k = kv[:, :width]
        v = kv[:, width:]
        kid = jnp.concatenate([kid_ref[kp] for kp in kps], axis=1)
        allowed = jnp.logical_and(qid == kid, slot_chunk + base < count)
        for h in range(heads):
            s = lax.dot_general(
                head_q[h], k, (((1,), (1,)), ((), ())), preferred_element_type=jnp.float32
            )
            s = jnp.where(allowed, s * scale, -jnp.inf)
            m_old = m_ref[h]
            m_new = jnp.maximum(m_old, jnp.max(s, axis=1, keepdims=True))
            p = jnp.exp(s - m_new)
            alpha = jnp.exp(m_old - m_new)
            l_ref[h] = alpha * l_ref[h] + jnp.sum(p, axis=1, keepdims=True)
            acc_ref[h] = alpha * acc_ref[h] + jnp.dot(
                p.astype(jnp.bfloat16), v, preferred_element_type=jnp.float32
            )
            m_ref[h] = m_new
        return carry

    lax.fori_loop(0, (count + CHUNK - 1) // CHUNK, body, 0)
    out = acc_ref[0] / l_ref[0]
    for h in range(1, heads):
        out = jnp.where(lane_head == h, acc_ref[h] / l_ref[h], out)
    o_ref[...] = out.astype(o_ref.dtype)


def paged_attention(queries, kv, slot_request, dp_rank):
    pages, page = slot_request.shape
    rows, width = queries.shape
    own_pages = rows // page
    heads = width // HEAD
    present = (
        slot_request[:, :, None] == jnp.arange(-1, 4, dtype=jnp.int32)[None, None, :]
    ).any(axis=1).astype(jnp.float32)
    own = lax.dynamic_slice_in_dim(present, dp_rank * own_pages, own_pages, 0)
    allowed = (jnp.dot(own, present.T) > 0).astype(jnp.int32)
    counts = jnp.sum(allowed, axis=1)
    visit = jnp.argsort(1 - allowed, axis=1, stable=True).astype(jnp.int32)
    visit = jnp.pad(visit, ((0, 0), (0, CHUNK)), mode="edge").reshape(-1)
    own_ids = lax.dynamic_slice_in_dim(slot_request, dp_rank * own_pages, own_pages, 0)
    qid = own_ids.reshape(rows, 1)
    kid = slot_request.reshape(pages, 1, page)
    kv3 = kv.reshape(pages, page, 2 * width)
    grid_spec = pltpu.PrefetchScalarGridSpec(
        num_scalar_prefetch=2,
        grid=(own_pages,),
        in_specs=[
            pl.BlockSpec((page, width), lambda i, a, n: (i, 0)),
            pl.BlockSpec((page, 1), lambda i, a, n: (i, 0)),
            pl.BlockSpec((pages, page, 2 * width), lambda i, a, n: (0, 0, 0)),
            pl.BlockSpec((pages, 1, page), lambda i, a, n: (0, 0, 0)),
        ],
        out_specs=pl.BlockSpec((page, width), lambda i, a, n: (i, 0)),
        scratch_shapes=[
            pltpu.VMEM((heads, page, 1), jnp.float32),
            pltpu.VMEM((heads, page, 1), jnp.float32),
            pltpu.VMEM((heads, page, width), jnp.float32),
        ],
    )
    return pl.pallas_call(
        attention_kernel,
        grid_spec=grid_spec,
        out_shape=jax.ShapeDtypeStruct((rows, width), jnp.bfloat16),
        interpret=INTERPRET,
    )(visit, counts, queries, qid, kv3, kid)


def shards(tokens, w_qkv, w_out, w_up, w_down, slot_request):
    groups = lax.axis_size("tensor")
    tensor_rank = lax.axis_index("tensor")
    qkv_block, up_block, down_block, out_full = spread_weights(w_qkv, w_out, w_up, w_down)
    tok_rows = tokens.shape[0]
    piece_rows = tok_rows // groups
    head_size = D // H
    heads_here = qkv_block.shape[1] // (3 * head_size)
    qkv = jnp.dot(tokens, qkv_block, preferred_element_type=jnp.float32).astype(jnp.bfloat16)
    qkv = qkv.reshape(tok_rows, heads_here, 3, head_size)
    queries = qkv[:, :, 0, :]
    key_rows = qkv[:, :, 1, :].reshape(tok_rows, heads_here * head_size)
    value_rows = qkv[:, :, 2, :].reshape(tok_rows, heads_here * head_size)
    slot_ids = slot_request.reshape(-1)
    own_ids = lax.dynamic_slice_in_dim(slot_ids, lax.axis_index("dp") * tok_rows, tok_rows, 0)

    kv_rows = jnp.concatenate([key_rows, value_rows], axis=1)
    kv_piece = lax.all_gather(kv_rows, "dp", axis=0, tiled=False)
    kv_piece, up_block, down_block, out_full = lax.optimization_barrier(
        (kv_piece, up_block, down_block, out_full)
    )
    attn = paged_attention(
        queries.reshape(tok_rows, heads_here * head_size),
        kv_piece,
        slot_request,
        lax.axis_index("dp"),
    )
    my_ids = lax.dynamic_slice_in_dim(own_ids, tensor_rank * piece_rows, piece_rows, 0)
    spread = jnp.broadcast_to(attn[None], (groups,) + attn.shape)
    heads_all = lax.all_to_all(spread, "tensor", 0, 2, tiled=True).reshape(tok_rows, -1)
    out_cols = out_full.reshape(-1, out_full.shape[3])
    proj = lax.dot_general(
        heads_all, out_cols, (((1,), (1,)), ((), ())), preferred_element_type=jnp.float32
    )
    first = layer_norm(tokens.astype(jnp.float32) + proj).astype(jnp.bfloat16)
    inner = jax.nn.gelu(
        jnp.dot(first, up_block, preferred_element_type=jnp.float32), approximate=False
    ).astype(jnp.bfloat16)
    down_cols = down_block.reshape(-1, down_block.shape[3])
    partial = lax.dot_general(
        inner, down_cols, (((1,), (1,)), ((), ())), preferred_element_type=jnp.float32
    )
    ffn = sum_scatter(partial.astype(jnp.bfloat16))
    first_rows = lax.dynamic_slice_in_dim(first, tensor_rank * piece_rows, piece_rows, 0)
    live = (my_ids >= 0).astype(jnp.float32)[:, None]
    encoded_rows = (layer_norm(first_rows.astype(jnp.float32) + ffn) * live).astype(jnp.bfloat16)
    return gather_rows(encoded_rows)


def solution(mesh):
    in_specs = (
        P("dp", None),
        P(("dp", "tensor"), None),
        P(None, ("dp", "tensor")),
        P(("dp", "tensor"), None),
        P(None, ("dp", "tensor")),
        P(),
    )
    out_specs = P("dp", None)
    return jax.shard_map(shards, mesh=mesh, in_specs=in_specs, out_specs=out_specs, check_vma=False)
```

```python
import functools
import math

import jax
import jax.numpy as jnp
from jax import lax
from jax.experimental import pallas as pl
from jax.experimental.pallas import tpu as pltpu
from jax.sharding import PartitionSpec as P


D = 1024
H = 16


def layer_norm(value):
    mean = jnp.mean(value, axis=-1, keepdims=True)
    centred = value - mean
    spread = jnp.mean(centred * centred, axis=-1, keepdims=True)
    return centred * lax.rsqrt(spread + 1e-05)


def spread_weights(w_qkv, w_out, w_up, w_down):
    groups = lax.axis_size("tensor")
    qkv = w_qkv.astype(jnp.bfloat16)
    up = w_up.astype(jnp.bfloat16)
    out_t = w_out.astype(jnp.bfloat16).T
    down_t = w_down.astype(jnp.bfloat16).T
    rows = qkv.shape[0]
    cols = out_t.shape[0]
    parts = [
        qkv.reshape(rows, groups, -1).transpose(1, 0, 2).reshape(groups, -1),
        up.reshape(rows, groups, -1).transpose(1, 0, 2).reshape(groups, -1),
        down_t.reshape(cols, groups, -1).transpose(1, 0, 2).reshape(groups, -1),
        jnp.broadcast_to(out_t.reshape(1, -1), (groups, out_t.size)),
    ]
    sizes = [p.shape[1] for p in parts]
    got = lax.all_to_all(jnp.concatenate(parts, axis=1), "tensor", 0, 0, tiled=True)
    cut = [sum(sizes[:k]) for k in range(5)]
    piece = [got[:, cut[k]:cut[k + 1]] for k in range(4)]
    qkv_local = piece[0].reshape(groups * rows, -1)
    width = up.shape[1] // groups
    up_local = piece[1].reshape(groups * rows, width)
    down_local = piece[2].reshape(-1, width)
    out_local = piece[3].reshape(-1, width)
    qkv_block = lax.all_gather(qkv_local, "dp", axis=0, tiled=True)
    rest = jnp.concatenate([up_local, down_local, out_local], axis=0)
    all_rest = lax.all_gather(rest, "dp", axis=0, tiled=False)
    dp_size = all_rest.shape[0]
    offs = [0, up_local.shape[0], up_local.shape[0] + down_local.shape[0], rest.shape[0]]
    up_block = all_rest[:, offs[0]:offs[1]].reshape(dp_size * up_local.shape[0], width)
    down_full = all_rest[:, offs[1]:offs[2]].reshape(dp_size, groups, cols, -1)
    out_full = all_rest[:, offs[2]:offs[3]].reshape(dp_size, groups, cols, -1)
    return qkv_block, up_block, down_full, out_full


def sum_scatter(part):
    groups = lax.axis_size("tensor")
    pieces = lax.all_to_all(part.reshape(groups, -1, part.shape[1]), "tensor", 0, 0, tiled=True)
    return jnp.sum(pieces.astype(jnp.float32), axis=0)


def gather_rows(rows):
    groups = lax.axis_size("tensor")
    spread = jnp.broadcast_to(rows[None], (groups,) + rows.shape)
    return lax.all_to_all(spread, "tensor", 0, 0, tiled=True).reshape(-1, rows.shape[1])


HEAD = D // H
INTERPRET = False
CHUNK = 16


def attention_kernel(first, last, list_ref, count_ref, q_ref, qid_ref, kv_ref, kid_ref, *refs):
    if first:
        outs = refs[:-3]
    else:
        m_in, l_in, acc_in = refs[:3]
        outs = refs[3:-3]
    m_ref, l_ref, acc_ref = refs[-3:]
    i = pl.program_id(0)
    pages = kv_ref.shape[0]
    page = kv_ref.shape[1]
    width = q_ref.shape[1]
    heads = width // HEAD
    scale = 1.0 / math.sqrt(HEAD)
    q = q_ref[...]
    lane_head = lax.broadcasted_iota(jnp.int32, q.shape, 1) // HEAD
    head_q = [jnp.where(lane_head == h, q, jnp.zeros_like(q)) for h in range(heads)]
    qid = qid_ref[...]
    count = count_ref[i]
    if first:
        m_ref[...] = jnp.full(m_ref.shape, -1e30, jnp.float32)
        l_ref[...] = jnp.zeros(l_ref.shape, jnp.float32)
        acc_ref[...] = jnp.zeros(acc_ref.shape, jnp.float32)
    else:
        m_ref[...] = m_in[...]
        l_ref[...] = l_in[...]
        acc_ref[...] = acc_in[...]
    slot_chunk = lax.broadcasted_iota(jnp.int32, (1, CHUNK * page), 1) // page

    def body(c, carry):
        base = c * CHUNK
        kps = [list_ref[i * (pages + CHUNK) + base + j] for j in range(CHUNK)]
        kv = jnp.concatenate([kv_ref[kp] for kp in kps], axis=0)
        k = kv[:, :width]
        v = kv[:, width:]
        kid = jnp.concatenate([kid_ref[kp] for kp in kps], axis=1)
        allowed = jnp.logical_and(qid == kid, slot_chunk + base < count)
        for h in range(heads):
            s = lax.dot_general(
                head_q[h], k, (((1,), (1,)), ((), ())), preferred_element_type=jnp.float32
            )
            s = jnp.where(allowed, s * scale, -jnp.inf)
            m_old = m_ref[h]
            m_new = jnp.maximum(m_old, jnp.max(s, axis=1, keepdims=True))
            p = jnp.exp(s - m_new)
            alpha = jnp.exp(m_old - m_new)
            l_ref[h] = alpha * l_ref[h] + jnp.sum(p, axis=1, keepdims=True)
            acc_ref[h] = alpha * acc_ref[h] + jnp.dot(
                p.astype(jnp.bfloat16), v, preferred_element_type=jnp.float32
            )
            m_ref[h] = m_new
        return carry

    lax.fori_loop(0, (count + CHUNK - 1) // CHUNK, body, 0)
    if last:
        out = acc_ref[0] / l_ref[0]
        for h in range(1, heads):
            out = jnp.where(lane_head == h, acc_ref[h] / l_ref[h], out)
        outs[0][...] = out.astype(outs[0].dtype)
    else:
        outs[0][...] = m_ref[...]
        outs[1][...] = l_ref[...]
        outs[2][...] = acc_ref[...]


def attention_pass(queries, kv, slot_request, dp_rank, part, parts, state):
    _, page = slot_request.shape
    rows, width = queries.shape
    own_pages = rows // page
    heads = width // HEAD
    dp_size = kv.shape[0]
    part_pages = own_pages // parts
    present = (
        slot_request[:, :, None] == jnp.arange(-1, 4, dtype=jnp.int32)[None, None, :]
    ).any(axis=1).astype(jnp.float32)
    own = lax.dynamic_slice_in_dim(present, dp_rank * own_pages, own_pages, 0)
    allowed = (jnp.dot(own, present.T) > 0).astype(jnp.int32)
    allowed = allowed.reshape(own_pages, dp_size, own_pages)[:, :, part * part_pages:(part + 1) * part_pages]
    allowed = allowed.reshape(own_pages, -1)
    counts = jnp.sum(allowed, axis=1)
    visit = jnp.argsort(1 - allowed, axis=1, stable=True).astype(jnp.int32)
    visit = jnp.pad(visit, ((0, 0), (0, CHUNK)), mode="edge").reshape(-1)
    own_ids = lax.dynamic_slice_in_dim(slot_request, dp_rank * own_pages, own_pages, 0)
    qid = own_ids.reshape(rows, 1)
    kid = slot_request.reshape(dp_size, own_pages, page)[:, part * part_pages:(part + 1) * part_pages]
    kid = kid.reshape(-1, 1, page)
    kv3 = kv.reshape(-1, page, 2 * width)
    seen = kv3.shape[0]
    first, last = part == 0, part == parts - 1
    row_spec = pl.BlockSpec((page, width), lambda i, a, n: (i, 0))
    state_specs = [
        pl.BlockSpec((heads, page, 1), lambda i, a, n: (0, i, 0)),
        pl.BlockSpec((heads, page, 1), lambda i, a, n: (0, i, 0)),
        pl.BlockSpec((heads, page, width), lambda i, a, n: (0, i, 0)),
    ]
    state_shapes = [
        jax.ShapeDtypeStruct((heads, rows, 1), jnp.float32),
        jax.ShapeDtypeStruct((heads, rows, 1), jnp.float32),
        jax.ShapeDtypeStruct((heads, rows, width), jnp.float32),
    ]
    in_specs = [
        row_spec,
        pl.BlockSpec((page, 1), lambda i, a, n: (i, 0)),
        pl.BlockSpec((seen, page, 2 * width), lambda i, a, n: (0, 0, 0)),
        pl.BlockSpec((seen, 1, page), lambda i, a, n: (0, 0, 0)),
    ]
    if not first:
        in_specs = in_specs + state_specs
    grid_spec = pltpu.PrefetchScalarGridSpec(
        num_scalar_prefetch=2,
        grid=(own_pages,),
        in_specs=in_specs,
        out_specs=[row_spec] if last else state_specs,
        scratch_shapes=[
            pltpu.VMEM((heads, page, 1), jnp.float32),
            pltpu.VMEM((heads, page, 1), jnp.float32),
            pltpu.VMEM((heads, page, width), jnp.float32),
        ],
    )
    out_shape = [jax.ShapeDtypeStruct((rows, width), jnp.bfloat16)] if last else state_shapes
    args = [visit, counts, queries, qid, kv3, kid] + ([] if first else list(state))
    result = pl.pallas_call(
        functools.partial(attention_kernel, first, last),
        grid_spec=grid_spec,
        out_shape=out_shape,
        interpret=INTERPRET,
    )(*args)
    return result[0] if last else result


def paged_attention(queries, kv_parts, slot_request, dp_rank):
    state = None
    parts = len(kv_parts)
    for part, kv in enumerate(kv_parts):
        state = attention_pass(queries, kv, slot_request, dp_rank, part, parts, state)
    return state


def shards(tokens, w_qkv, w_out, w_up, w_down, slot_request):
    groups = lax.axis_size("tensor")
    tensor_rank = lax.axis_index("tensor")
    qkv_block, up_block, down_block, out_full = spread_weights(w_qkv, w_out, w_up, w_down)
    tok_rows = tokens.shape[0]
    piece_rows = tok_rows // groups
    head_size = D // H
    heads_here = qkv_block.shape[1] // (3 * head_size)
    qkv = jnp.dot(tokens, qkv_block, preferred_element_type=jnp.float32).astype(jnp.bfloat16)
    qkv = qkv.reshape(tok_rows, heads_here, 3, head_size)
    queries = qkv[:, :, 0, :]
    key_rows = qkv[:, :, 1, :].reshape(tok_rows, heads_here * head_size)
    value_rows = qkv[:, :, 2, :].reshape(tok_rows, heads_here * head_size)
    slot_ids = slot_request.reshape(-1)
    own_ids = lax.dynamic_slice_in_dim(slot_ids, lax.axis_index("dp") * tok_rows, tok_rows, 0)

    kv_rows = jnp.concatenate([key_rows, value_rows], axis=1)
    kv_rows, up_block, down_block, out_full = lax.optimization_barrier(
        (kv_rows, up_block, down_block, out_full)
    )
    parts = 2
    part_rows = tok_rows // parts
    kv_parts = []
    for p in range(parts):
        kv_parts.append(
            lax.all_gather(kv_rows[p * part_rows:(p + 1) * part_rows], "dp", axis=0, tiled=False)
        )
    attn = paged_attention(
        queries.reshape(tok_rows, heads_here * head_size),
        kv_parts,
        slot_request,
        lax.axis_index("dp"),
    )
    my_ids = lax.dynamic_slice_in_dim(own_ids, tensor_rank * piece_rows, piece_rows, 0)
    spread = jnp.broadcast_to(attn[None], (groups,) + attn.shape)
    heads_all = lax.all_to_all(spread, "tensor", 0, 2, tiled=True).reshape(tok_rows, -1)
    out_cols = out_full.reshape(-1, out_full.shape[3])
    proj = lax.dot_general(
        heads_all, out_cols, (((1,), (1,)), ((), ())), preferred_element_type=jnp.float32
    )
    first = layer_norm(tokens.astype(jnp.float32) + proj).astype(jnp.bfloat16)
    inner = jax.nn.gelu(
        jnp.dot(first, up_block, preferred_element_type=jnp.float32), approximate=False
    ).astype(jnp.bfloat16)
    down_cols = down_block.reshape(-1, down_block.shape[3])
    partial = lax.dot_general(
        inner, down_cols, (((1,), (1,)), ((), ())), preferred_element_type=jnp.float32
    )
    ffn = sum_scatter(partial.astype(jnp.bfloat16))
    first_rows = lax.dynamic_slice_in_dim(first, tensor_rank * piece_rows, piece_rows, 0)
    live = (my_ids >= 0).astype(jnp.float32)[:, None]
    encoded_rows = (layer_norm(first_rows.astype(jnp.float32) + ffn) * live).astype(jnp.bfloat16)
    return gather_rows(encoded_rows)


def solution(mesh):
    in_specs = (
        P("dp", None),
        P(("dp", "tensor"), None),
        P(None, ("dp", "tensor")),
        P(("dp", "tensor"), None),
        P(None, ("dp", "tensor")),
        P(),
    )
    out_specs = P("dp", None)

    return jax.shard_map(shards, mesh=mesh, in_specs=in_specs, out_specs=out_specs, check_vma=False)
```

```python
import math

import jax
import jax.numpy as jnp
from jax import lax
from jax.experimental import pallas as pl
from jax.experimental.pallas import tpu as pltpu
from jax.sharding import PartitionSpec as P

D = 1024
H = 16


def layer_norm(value):
    mean = jnp.mean(value, axis=-1, keepdims=True)
    centred = value - mean
    spread = jnp.mean(centred * centred, axis=-1, keepdims=True)
    return centred * lax.rsqrt(spread + 1e-05)


def spread_weights(w_qkv, w_out, w_up, w_down):
    groups = lax.axis_size("tensor")
    qkv = w_qkv.astype(jnp.bfloat16)
    up = w_up.astype(jnp.bfloat16)
    out_t = w_out.astype(jnp.bfloat16).T
    down_t = w_down.astype(jnp.bfloat16).T
    rows = qkv.shape[0]
    cols = out_t.shape[0]
    parts = [
        qkv.reshape(rows, groups, -1).transpose(1, 0, 2).reshape(groups, -1),
        up.reshape(rows, groups, -1).transpose(1, 0, 2).reshape(groups, -1),
        down_t.reshape(cols, groups, -1).transpose(1, 0, 2).reshape(groups, -1),
        jnp.broadcast_to(out_t.reshape(1, -1), (groups, out_t.size)),
    ]
    sizes = [p.shape[1] for p in parts]
    got = lax.all_to_all(jnp.concatenate(parts, axis=1), "tensor", 0, 0, tiled=True)
    cut = [sum(sizes[:k]) for k in range(5)]
    piece = [got[:, cut[k]:cut[k + 1]] for k in range(4)]
    qkv_local = piece[0].reshape(groups * rows, -1)
    width = up.shape[1] // groups
    up_local = piece[1].reshape(groups * rows, width)
    down_local = piece[2].reshape(-1, width)
    out_local = piece[3].reshape(-1, width)
    qkv_block = lax.all_gather(qkv_local, "dp", axis=0, tiled=True)
    rest = jnp.concatenate([up_local, down_local, out_local], axis=0)
    all_rest = lax.all_gather(rest, "dp", axis=0, tiled=False)
    dp_size = all_rest.shape[0]
    offs = [0, up_local.shape[0], up_local.shape[0] + down_local.shape[0], rest.shape[0]]
    up_block = all_rest[:, offs[0]:offs[1]].reshape(dp_size * up_local.shape[0], width)
    down_full = all_rest[:, offs[1]:offs[2]].reshape(dp_size, groups, cols, -1)
    out_full = all_rest[:, offs[2]:offs[3]].reshape(dp_size, groups, cols, -1)
    return qkv_block, up_block, down_full, out_full


def sum_scatter(part):
    groups = lax.axis_size("tensor")
    pieces = lax.all_to_all(part.reshape(groups, -1, part.shape[1]), "tensor", 0, 0, tiled=True)
    return jnp.sum(pieces.astype(jnp.float32), axis=0)


def gather_rows(rows):
    groups = lax.axis_size("tensor")
    spread = jnp.broadcast_to(rows[None], (groups,) + rows.shape)
    return lax.all_to_all(spread, "tensor", 0, 0, tiled=True).reshape(-1, rows.shape[1])


HEAD = D // H
INTERPRET = False
CHUNK = 24


def attention_kernel(list_ref, count_ref, q_ref, qid_ref, kv_ref, kid_ref, o_ref, m_ref, l_ref, acc_ref):
    i = pl.program_id(0)
    pages = kv_ref.shape[0]
    page = kv_ref.shape[1]
    width = q_ref.shape[1]
    heads = width // HEAD
    scale = 1.0 / math.sqrt(HEAD)
    q = q_ref[...]
    lane_head = lax.broadcasted_iota(jnp.int32, q.shape, 1) // HEAD
    stacked_q = jnp.concatenate(
        [jnp.where(lane_head == h, q, jnp.zeros_like(q)) for h in range(heads)], axis=0
    )
    qid = qid_ref[...]
    stacked_id = jnp.concatenate([qid] * heads, axis=0)
    count = count_ref[i]
    m_ref[...] = jnp.full(m_ref.shape, -1e30, jnp.float32)
    l_ref[...] = jnp.zeros(l_ref.shape, jnp.float32)
    acc_ref[...] = jnp.zeros(acc_ref.shape, jnp.float32)
    slot_chunk = lax.broadcasted_iota(jnp.int32, (1, CHUNK * page), 1) // page

    def body(c, carry):
        base = c * CHUNK
        kps = [list_ref[i * (pages + CHUNK) + base + j] for j in range(CHUNK)]
        kv = jnp.concatenate([kv_ref[kp] for kp in kps], axis=0)
        k = kv[:, :width]
        v = kv[:, width:]
        kid = jnp.concatenate([kid_ref[kp] for kp in kps], axis=1)
        allowed = jnp.logical_and(stacked_id == kid, slot_chunk + base < count)
        s = lax.dot_general(
            stacked_q, k, (((1,), (1,)), ((), ())), preferred_element_type=jnp.float32
        )
        s = jnp.where(allowed, s * scale, -jnp.inf)
        m_old = m_ref[...]
        m_new = jnp.maximum(m_old, jnp.max(s, axis=1, keepdims=True))
        p = jnp.exp(s - m_new)
        alpha = jnp.exp(m_old - m_new)
        l_ref[...] = alpha * l_ref[...] + jnp.sum(p, axis=1, keepdims=True)
        acc_ref[...] = alpha * acc_ref[...] + jnp.dot(
            p.astype(jnp.bfloat16), v, preferred_element_type=jnp.float32
        )
        m_ref[...] = m_new
        return carry

    lax.fori_loop(0, (count + CHUNK - 1) // CHUNK, body, 0)
    rows = q.shape[0]
    out = acc_ref[0:rows] / l_ref[0:rows]
    for h in range(1, heads):
        out = jnp.where(
            lane_head == h, acc_ref[h * rows:(h + 1) * rows] / l_ref[h * rows:(h + 1) * rows], out
        )
    o_ref[...] = out.astype(o_ref.dtype)


def paged_attention(queries, kv, slot_request, dp_rank):
    pages, page = slot_request.shape
    rows, width = queries.shape
    own_pages = rows // page
    heads = width // HEAD
    present = (
        slot_request[:, :, None] == jnp.arange(-1, 4, dtype=jnp.int32)[None, None, :]
    ).any(axis=1).astype(jnp.float32)
    own = lax.dynamic_slice_in_dim(present, dp_rank * own_pages, own_pages, 0)
    allowed = (jnp.dot(own, present.T) > 0).astype(jnp.int32)
    counts = jnp.sum(allowed, axis=1)
    visit = jnp.argsort(1 - allowed, axis=1, stable=True).astype(jnp.int32)
    visit = jnp.pad(visit, ((0, 0), (0, CHUNK)), mode="edge").reshape(-1)
    own_ids = lax.dynamic_slice_in_dim(slot_request, dp_rank * own_pages, own_pages, 0)
    qid = own_ids.reshape(rows, 1)
    kid = slot_request.reshape(pages, 1, page)
    kv3 = kv.reshape(pages, page, 2 * width)
    grid_spec = pltpu.PrefetchScalarGridSpec(
        num_scalar_prefetch=2,
        grid=(own_pages,),
        in_specs=[
            pl.BlockSpec((page, width), lambda i, a, n: (i, 0)),
            pl.BlockSpec((page, 1), lambda i, a, n: (i, 0)),
            pl.BlockSpec((pages, page, 2 * width), lambda i, a, n: (0, 0, 0)),
            pl.BlockSpec((pages, 1, page), lambda i, a, n: (0, 0, 0)),
        ],
        out_specs=pl.BlockSpec((page, width), lambda i, a, n: (i, 0)),
        scratch_shapes=[
            pltpu.VMEM((heads * page, 1), jnp.float32),
            pltpu.VMEM((heads * page, 1), jnp.float32),
            pltpu.VMEM((heads * page, width), jnp.float32),
        ],
    )
    return pl.pallas_call(
        attention_kernel,
        grid_spec=grid_spec,
        out_shape=jax.ShapeDtypeStruct((rows, width), jnp.bfloat16),
        interpret=INTERPRET,
    )(visit, counts, queries, qid, kv3, kid)


def shards(tokens, w_qkv, w_out, w_up, w_down, slot_request):
    groups = lax.axis_size("tensor")
    tensor_rank = lax.axis_index("tensor")
    qkv_block, up_block, down_block, out_full = spread_weights(w_qkv, w_out, w_up, w_down)
    tok_rows = tokens.shape[0]
    piece_rows = tok_rows // groups
    head_size = D // H
    heads_here = qkv_block.shape[1] // (3 * head_size)
    qkv = jnp.dot(tokens, qkv_block, preferred_element_type=jnp.float32).astype(jnp.bfloat16)
    qkv = qkv.reshape(tok_rows, heads_here, 3, head_size)
    queries = qkv[:, :, 0, :]
    key_rows = qkv[:, :, 1, :].reshape(tok_rows, heads_here * head_size)
    value_rows = qkv[:, :, 2, :].reshape(tok_rows, heads_here * head_size)
    slot_ids = slot_request.reshape(-1)
    own_ids = lax.dynamic_slice_in_dim(slot_ids, lax.axis_index("dp") * tok_rows, tok_rows, 0)

    kv_rows = jnp.concatenate([key_rows, value_rows], axis=1)
    kv_piece = lax.all_gather(kv_rows, "dp", axis=0, tiled=False)
    kv_piece, up_block, down_block, out_full = lax.optimization_barrier(
        (kv_piece, up_block, down_block, out_full)
    )
    attn = paged_attention(
        queries.reshape(tok_rows, heads_here * head_size),
        kv_piece,
        slot_request,
        lax.axis_index("dp"),
    )
    my_ids = lax.dynamic_slice_in_dim(own_ids, tensor_rank * piece_rows, piece_rows, 0)
    spread = jnp.broadcast_to(attn[None], (groups,) + attn.shape)
    heads_all = lax.all_to_all(spread, "tensor", 0, 2, tiled=True).reshape(tok_rows, -1)
    out_cols = out_full.reshape(-1, out_full.shape[3])
    proj = lax.dot_general(
        heads_all, out_cols, (((1,), (1,)), ((), ())), preferred_element_type=jnp.float32
    )
    first = layer_norm(tokens.astype(jnp.float32) + proj).astype(jnp.bfloat16)
    inner = jax.nn.gelu(
        jnp.dot(first, up_block, preferred_element_type=jnp.float32), approximate=False
    ).astype(jnp.bfloat16)
    down_cols = down_block.reshape(-1, down_block.shape[3])
    partial = lax.dot_general(
        inner, down_cols, (((1,), (1,)), ((), ())), preferred_element_type=jnp.float32
    )
    ffn = sum_scatter(partial.astype(jnp.bfloat16))
    first_rows = lax.dynamic_slice_in_dim(first, tensor_rank * piece_rows, piece_rows, 0)
    live = (my_ids >= 0).astype(jnp.float32)[:, None]
    encoded_rows = (layer_norm(first_rows.astype(jnp.float32) + ffn) * live).astype(jnp.bfloat16)
    return gather_rows(encoded_rows)


def solution(mesh):
    in_specs = (
        P("dp", None),
        P(("dp", "tensor"), None),
        P(None, ("dp", "tensor")),
        P(("dp", "tensor"), None),
        P(None, ("dp", "tensor")),
        P(),
    )
    out_specs = P("dp", None)
    return jax.shard_map(shards, mesh=mesh, in_specs=in_specs, out_specs=out_specs, check_vma=False)
```

```python
import math

import jax
import jax.numpy as jnp
from jax import lax
from jax.experimental import pallas as pl
from jax.experimental.pallas import tpu as pltpu
from jax.sharding import PartitionSpec as P

D = 1024
H = 16


def layer_norm(value):
    mean = jnp.mean(value, axis=-1, keepdims=True)
    centred = value - mean
    spread = jnp.mean(centred * centred, axis=-1, keepdims=True)
    return centred * lax.rsqrt(spread + 1e-05)


def spread_weights(w_qkv, w_out, w_up, w_down):
    groups = lax.axis_size("tensor")
    qkv = w_qkv.astype(jnp.bfloat16)
    up = w_up.astype(jnp.bfloat16)
    out_t = w_out.astype(jnp.bfloat16).T
    down_t = w_down.astype(jnp.bfloat16).T
    rows = qkv.shape[0]
    cols = out_t.shape[0]
    parts = [
        qkv.reshape(rows, groups, -1).transpose(1, 0, 2).reshape(groups, -1),
        up.reshape(rows, groups, -1).transpose(1, 0, 2).reshape(groups, -1),
        down_t.reshape(cols, groups, -1).transpose(1, 0, 2).reshape(groups, -1),
        jnp.broadcast_to(out_t.reshape(1, -1), (groups, out_t.size)),
    ]
    sizes = [p.shape[1] for p in parts]
    got = lax.all_to_all(jnp.concatenate(parts, axis=1), "tensor", 0, 0, tiled=True)
    cut = [sum(sizes[:k]) for k in range(5)]
    piece = [got[:, cut[k]:cut[k + 1]] for k in range(4)]
    qkv_local = piece[0].reshape(groups * rows, -1)
    width = up.shape[1] // groups
    up_local = piece[1].reshape(groups * rows, width)
    down_local = piece[2].reshape(-1, width)
    out_local = piece[3].reshape(-1, width)
    qkv_block = lax.all_gather(qkv_local, "dp", axis=0, tiled=True)
    rest = jnp.concatenate([up_local, down_local, out_local], axis=0)
    all_rest = lax.all_gather(rest, "dp", axis=0, tiled=False)
    dp_size = all_rest.shape[0]
    offs = [0, up_local.shape[0], up_local.shape[0] + down_local.shape[0], rest.shape[0]]
    up_block = all_rest[:, offs[0]:offs[1]].reshape(dp_size * up_local.shape[0], width)
    down_full = all_rest[:, offs[1]:offs[2]].reshape(dp_size, groups, cols, -1)
    out_full = all_rest[:, offs[2]:offs[3]].reshape(dp_size, groups, cols, -1)
    return qkv_block, up_block, down_full, out_full


def sum_scatter(part):
    groups = lax.axis_size("tensor")
    pieces = lax.all_to_all(part.reshape(groups, -1, part.shape[1]), "tensor", 0, 0, tiled=True)
    return jnp.sum(pieces.astype(jnp.float32), axis=0)


def gather_rows(rows):
    groups = lax.axis_size("tensor")
    spread = jnp.broadcast_to(rows[None], (groups,) + rows.shape)
    return lax.all_to_all(spread, "tensor", 0, 0, tiled=True).reshape(-1, rows.shape[1])


HEAD = D // H
INTERPRET = False
CHUNK = 24


def attention_kernel(list_ref, count_ref, q_ref, qid_ref, kv_ref, kid_ref, o_ref, m_ref, l_ref, acc_ref):
    i = pl.program_id(0)
    pages = kv_ref.shape[0]
    page = kv_ref.shape[1]
    width = q_ref.shape[1]
    heads = width // HEAD
    scale = 1.0 / math.sqrt(HEAD)
    q = q_ref[...]
    lane_head = lax.broadcasted_iota(jnp.int32, q.shape, 1) // HEAD
    stacked_q = jnp.concatenate(
        [jnp.where(lane_head == h, q, jnp.zeros_like(q)) for h in range(heads)], axis=0
    )
    qid = qid_ref[...]
    stacked_id = jnp.concatenate([qid] * heads, axis=0)
    count = count_ref[i]
    m_ref[...] = jnp.full(m_ref.shape, -1e30, jnp.float32)
    l_ref[...] = jnp.zeros(l_ref.shape, jnp.float32)
    acc_ref[...] = jnp.zeros(acc_ref.shape, jnp.float32)
    slot_chunk = lax.broadcasted_iota(jnp.int32, (1, CHUNK * page), 1) // page

    def body(c, carry):
        base = c * CHUNK
        kps = [list_ref[i * (pages + CHUNK) + base + j] for j in range(CHUNK)]
        kv = jnp.concatenate([kv_ref[kp] for kp in kps], axis=0)
        k = kv[:, :width]
        v = kv[:, width:]
        kid = jnp.concatenate([kid_ref[kp] for kp in kps], axis=1)
        allowed = jnp.logical_and(stacked_id == kid, slot_chunk + base < count)
        s = lax.dot_general(
            stacked_q, k, (((1,), (1,)), ((), ())), preferred_element_type=jnp.float32
        )
        s = jnp.where(allowed, s * scale, -jnp.inf)
        m_old = m_ref[...]
        m_new = jnp.maximum(m_old, jnp.max(s, axis=1, keepdims=True))
        p = jnp.exp(s - m_new)
        alpha = jnp.exp(m_old - m_new)
        l_ref[...] = alpha * l_ref[...] + jnp.sum(p, axis=1, keepdims=True)
        acc_ref[...] = alpha * acc_ref[...] + jnp.dot(
            p.astype(jnp.bfloat16), v, preferred_element_type=jnp.float32
        )
        m_ref[...] = m_new
        return carry

    lax.fori_loop(0, (count + CHUNK - 1) // CHUNK, body, 0)
    rows = q.shape[0]
    out = acc_ref[0:rows] / l_ref[0:rows]
    for h in range(1, heads):
        out = jnp.where(
            lane_head == h, acc_ref[h * rows:(h + 1) * rows] / l_ref[h * rows:(h + 1) * rows], out
        )
    o_ref[...] = out.astype(o_ref.dtype)


def paged_attention(queries, kv, slot_request, dp_rank):
    pages, page = slot_request.shape
    rows, width = queries.shape
    own_pages = rows // page
    heads = width // HEAD
    present = (
        slot_request[:, :, None] == jnp.arange(-1, 4, dtype=jnp.int32)[None, None, :]
    ).any(axis=1).astype(jnp.float32)
    own = lax.dynamic_slice_in_dim(present, dp_rank * own_pages, own_pages, 0)
    allowed = (jnp.dot(own, present.T) > 0).astype(jnp.int32)
    counts = jnp.sum(allowed, axis=1)
    visit = jnp.argsort(1 - allowed, axis=1, stable=True).astype(jnp.int32)
    visit = jnp.pad(visit, ((0, 0), (0, CHUNK)), mode="edge").reshape(-1)
    own_ids = lax.dynamic_slice_in_dim(slot_request, dp_rank * own_pages, own_pages, 0)
    qid = own_ids.reshape(rows, 1)
    kid = slot_request.reshape(pages, 1, page)
    kv3 = kv.reshape(pages, page, 2 * width)
    grid_spec = pltpu.PrefetchScalarGridSpec(
        num_scalar_prefetch=2,
        grid=(own_pages,),
        in_specs=[
            pl.BlockSpec((page, width), lambda i, a, n: (i, 0)),
            pl.BlockSpec((page, 1), lambda i, a, n: (i, 0)),
            pl.BlockSpec((pages, page, 2 * width), lambda i, a, n: (0, 0, 0)),
            pl.BlockSpec((pages, 1, page), lambda i, a, n: (0, 0, 0)),
        ],
        out_specs=pl.BlockSpec((page, width), lambda i, a, n: (i, 0)),
        scratch_shapes=[
            pltpu.VMEM((heads * page, 1), jnp.float32),
            pltpu.VMEM((heads * page, 1), jnp.float32),
            pltpu.VMEM((heads * page, width), jnp.float32),
        ],
    )
    return pl.pallas_call(
        attention_kernel,
        grid_spec=grid_spec,
        out_shape=jax.ShapeDtypeStruct((rows, width), jnp.bfloat16),
        interpret=INTERPRET,
    )(visit, counts, queries, qid, kv3, kid)


def shards(tokens, w_qkv, w_out, w_up, w_down, slot_request):
    groups = lax.axis_size("tensor")
    tensor_rank = lax.axis_index("tensor")
    qkv_block, up_block, down_block, out_full = spread_weights(w_qkv, w_out, w_up, w_down)
    tok_rows = tokens.shape[0]
    piece_rows = tok_rows // groups
    head_size = D // H
    heads_here = qkv_block.shape[1] // (3 * head_size)
    qkv = jnp.dot(tokens, qkv_block, preferred_element_type=jnp.float32).astype(jnp.bfloat16)
    qkv = qkv.reshape(tok_rows, heads_here, 3, head_size)
    queries = qkv[:, :, 0, :]
    key_rows = qkv[:, :, 1, :].reshape(tok_rows, heads_here * head_size)
    value_rows = qkv[:, :, 2, :].reshape(tok_rows, heads_here * head_size)
    slot_ids = slot_request.reshape(-1)
    own_ids = lax.dynamic_slice_in_dim(slot_ids, lax.axis_index("dp") * tok_rows, tok_rows, 0)

    kv_rows = jnp.concatenate([key_rows, value_rows], axis=1)
    kv_piece = lax.all_gather(kv_rows, "dp", axis=0, tiled=False)
    attn = paged_attention(
        queries.reshape(tok_rows, heads_here * head_size),
        kv_piece,
        slot_request,
        lax.axis_index("dp"),
    )
    my_ids = lax.dynamic_slice_in_dim(own_ids, tensor_rank * piece_rows, piece_rows, 0)
    spread = jnp.broadcast_to(attn[None], (groups,) + attn.shape)
    heads_all = lax.all_to_all(spread, "tensor", 0, 2, tiled=True).reshape(tok_rows, -1)
    out_cols = out_full.reshape(-1, out_full.shape[3])
    proj = lax.dot_general(
        heads_all, out_cols, (((1,), (1,)), ((), ())), preferred_element_type=jnp.float32
    )
    first = layer_norm(tokens.astype(jnp.float32) + proj).astype(jnp.bfloat16)
    inner = jax.nn.gelu(
        jnp.dot(first, up_block, preferred_element_type=jnp.float32), approximate=False
    ).astype(jnp.bfloat16)
    down_cols = down_block.reshape(-1, down_block.shape[3])
    partial = lax.dot_general(
        inner, down_cols, (((1,), (1,)), ((), ())), preferred_element_type=jnp.float32
    )
    ffn = sum_scatter(partial.astype(jnp.bfloat16))
    first_rows = lax.dynamic_slice_in_dim(first, tensor_rank * piece_rows, piece_rows, 0)
    live = (my_ids >= 0).astype(jnp.float32)[:, None]
    encoded_rows = (layer_norm(first_rows.astype(jnp.float32) + ffn) * live).astype(jnp.bfloat16)
    return gather_rows(encoded_rows)


def solution(mesh):
    in_specs = (
        P("dp", None),
        P(("dp", "tensor"), None),
        P(None, ("dp", "tensor")),
        P(("dp", "tensor"), None),
        P(None, ("dp", "tensor")),
        P(),
    )
    out_specs = P("dp", None)
    return jax.shard_map(shards, mesh=mesh, in_specs=in_specs, out_specs=out_specs, check_vma=False)
```

```python
import math

import jax
import jax.numpy as jnp
from jax import lax
from jax.experimental import pallas as pl
from jax.experimental.pallas import tpu as pltpu
from jax.sharding import PartitionSpec as P

D = 1024
H = 16


def layer_norm(value):
    mean = jnp.mean(value, axis=-1, keepdims=True)
    centred = value - mean
    spread = jnp.mean(centred * centred, axis=-1, keepdims=True)
    return centred * lax.rsqrt(spread + 1e-05)


def spread_weights(w_qkv, w_out, w_up, w_down):
    groups = lax.axis_size("tensor")
    qkv = w_qkv.astype(jnp.bfloat16)
    up = w_up.astype(jnp.bfloat16)
    out_t = w_out.astype(jnp.bfloat16).T
    down_t = w_down.astype(jnp.bfloat16).T
    rows = qkv.shape[0]
    cols = out_t.shape[0]
    parts = [
        qkv.reshape(rows, groups, -1).transpose(1, 0, 2).reshape(groups, -1),
        up.reshape(rows, groups, -1).transpose(1, 0, 2).reshape(groups, -1),
        down_t.reshape(cols, groups, -1).transpose(1, 0, 2).reshape(groups, -1),
        jnp.broadcast_to(out_t.reshape(1, -1), (groups, out_t.size)),
    ]
    sizes = [p.shape[1] for p in parts]
    got = lax.all_to_all(jnp.concatenate(parts, axis=1), "tensor", 0, 0, tiled=True)
    cut = [sum(sizes[:k]) for k in range(5)]
    piece = [got[:, cut[k]:cut[k + 1]] for k in range(4)]
    qkv_local = piece[0].reshape(groups * rows, -1)
    width = up.shape[1] // groups
    up_local = piece[1].reshape(groups * rows, width)
    down_local = piece[2].reshape(-1, width)
    out_local = piece[3].reshape(-1, width)
    qkv_block = lax.all_gather(qkv_local, "dp", axis=0, tiled=True)
    rest = jnp.concatenate([up_local, down_local, out_local], axis=0)
    all_rest = lax.all_gather(rest, "dp", axis=0, tiled=False)
    dp_size = all_rest.shape[0]
    offs = [0, up_local.shape[0], up_local.shape[0] + down_local.shape[0], rest.shape[0]]
    up_block = all_rest[:, offs[0]:offs[1]].reshape(dp_size * up_local.shape[0], width)
    down_full = all_rest[:, offs[1]:offs[2]].reshape(dp_size, groups, cols, -1)
    out_full = all_rest[:, offs[2]:offs[3]].reshape(dp_size, groups, cols, -1)
    return qkv_block, up_block, down_full, out_full


def sum_scatter(part):
    groups = lax.axis_size("tensor")
    pieces = lax.all_to_all(part.reshape(groups, -1, part.shape[1]), "tensor", 0, 0, tiled=True)
    return jnp.sum(pieces.astype(jnp.float32), axis=0)


def gather_rows(rows):
    groups = lax.axis_size("tensor")
    spread = jnp.broadcast_to(rows[None], (groups,) + rows.shape)
    return lax.all_to_all(spread, "tensor", 0, 0, tiled=True).reshape(-1, rows.shape[1])


HEAD = D // H
INTERPRET = False
CHUNK = 24


def attention_kernel(list_ref, count_ref, q_ref, qid_ref, kv_ref, kid_ref, o_ref, m_ref, l_ref, acc_ref):
    i = pl.program_id(0)
    pages = kv_ref.shape[0]
    page = kv_ref.shape[1]
    width = q_ref.shape[1]
    heads = width // HEAD
    scale = 1.0 / math.sqrt(HEAD)
    q = q_ref[...]
    lane_head = lax.broadcasted_iota(jnp.int32, q.shape, 1) // HEAD
    stacked_q = jnp.concatenate(
        [jnp.where(lane_head == h, q, jnp.zeros_like(q)) for h in range(heads)], axis=0
    )
    qid = qid_ref[...]
    stacked_id = jnp.concatenate([qid] * heads, axis=0)
    count = count_ref[i]
    m_ref[...] = jnp.full(m_ref.shape, -1e30, jnp.float32)
    l_ref[...] = jnp.zeros(l_ref.shape, jnp.float32)
    acc_ref[...] = jnp.zeros(acc_ref.shape, jnp.float32)
    slot_chunk = lax.broadcasted_iota(jnp.int32, (1, CHUNK * page), 1) // page

    def body(c, carry):
        base = c * CHUNK
        kps = [list_ref[i * (pages + CHUNK) + base + j] for j in range(CHUNK)]
        kv = jnp.concatenate([kv_ref[kp] for kp in kps], axis=0)
        k = kv[:, :width]
        v = kv[:, width:]
        kid = jnp.concatenate([kid_ref[kp] for kp in kps], axis=1)
        allowed = jnp.logical_and(stacked_id == kid, slot_chunk + base < count)
        s = lax.dot_general(
            stacked_q, k, (((1,), (1,)), ((), ())), preferred_element_type=jnp.float32
        )
        s = jnp.where(allowed, s * scale, -jnp.inf)
        m_old = m_ref[...]
        m_new = jnp.maximum(m_old, jnp.max(s, axis=1, keepdims=True))
        p = jnp.exp(s - m_new)
        alpha = jnp.exp(m_old - m_new)
        l_ref[...] = alpha * l_ref[...] + jnp.sum(p, axis=1, keepdims=True)
        acc_ref[...] = alpha * acc_ref[...] + jnp.dot(
            p.astype(jnp.bfloat16), v, preferred_element_type=jnp.float32
        )
        m_ref[...] = m_new
        return carry

    lax.fori_loop(0, (count + CHUNK - 1) // CHUNK, body, 0)
    rows = q.shape[0]
    out = acc_ref[0:rows] / l_ref[0:rows]
    for h in range(1, heads):
        out = jnp.where(
            lane_head == h, acc_ref[h * rows:(h + 1) * rows] / l_ref[h * rows:(h + 1) * rows], out
        )
    o_ref[...] = out.astype(o_ref.dtype)


def paged_attention(queries, kv, slot_request, dp_rank):
    pages, page = slot_request.shape
    rows, width = queries.shape
    own_pages = rows // page
    heads = width // HEAD
    present = (
        slot_request[:, :, None] == jnp.arange(-1, 4, dtype=jnp.int32)[None, None, :]
    ).any(axis=1).astype(jnp.float32)
    own = lax.dynamic_slice_in_dim(present, dp_rank * own_pages, own_pages, 0)
    allowed = (jnp.dot(own, present.T) > 0).astype(jnp.int32)
    counts = jnp.sum(allowed, axis=1)
    visit = jnp.argsort(1 - allowed, axis=1, stable=True).astype(jnp.int32)
    visit = jnp.pad(visit, ((0, 0), (0, CHUNK)), mode="edge").reshape(-1)
    own_ids = lax.dynamic_slice_in_dim(slot_request, dp_rank * own_pages, own_pages, 0)
    qid = own_ids.reshape(rows, 1)
    kid = slot_request.reshape(pages, 1, page)
    kv3 = kv.reshape(pages, page, 2 * width)
    grid_spec = pltpu.PrefetchScalarGridSpec(
        num_scalar_prefetch=2,
        grid=(own_pages,),
        in_specs=[
            pl.BlockSpec((page, width), lambda i, a, n: (i, 0)),
            pl.BlockSpec((page, 1), lambda i, a, n: (i, 0)),
            pl.BlockSpec((pages, page, 2 * width), lambda i, a, n: (0, 0, 0)),
            pl.BlockSpec((pages, 1, page), lambda i, a, n: (0, 0, 0)),
        ],
        out_specs=pl.BlockSpec((page, width), lambda i, a, n: (i, 0)),
        scratch_shapes=[
            pltpu.VMEM((heads * page, 1), jnp.float32),
            pltpu.VMEM((heads * page, 1), jnp.float32),
            pltpu.VMEM((heads * page, width), jnp.float32),
        ],
    )
    return pl.pallas_call(
        attention_kernel,
        grid_spec=grid_spec,
        out_shape=jax.ShapeDtypeStruct((rows, width), jnp.bfloat16),
        interpret=INTERPRET,
    )(visit, counts, queries, qid, kv3, kid)


def shards(tokens, w_qkv, w_out, w_up, w_down, slot_request):
    groups = lax.axis_size("tensor")
    tensor_rank = lax.axis_index("tensor")
    qkv_block, up_block, down_block, out_full = spread_weights(w_qkv, w_out, w_up, w_down)
    tok_rows = tokens.shape[0]
    piece_rows = tok_rows // groups
    head_size = D // H
    heads_here = qkv_block.shape[1] // (3 * head_size)
    qkv = jnp.dot(tokens, qkv_block, preferred_element_type=jnp.float32).astype(jnp.bfloat16)
    qkv = qkv.reshape(tok_rows, heads_here, 3, head_size)
    queries = qkv[:, :, 0, :]
    key_rows = qkv[:, :, 1, :].reshape(tok_rows, heads_here * head_size)
    value_rows = qkv[:, :, 2, :].reshape(tok_rows, heads_here * head_size)
    slot_ids = slot_request.reshape(-1)
    own_ids = lax.dynamic_slice_in_dim(slot_ids, lax.axis_index("dp") * tok_rows, tok_rows, 0)

    kv_rows = jnp.concatenate([key_rows, value_rows], axis=1)
    kv_piece = lax.optimization_barrier(lax.all_gather(kv_rows, "dp", axis=0, tiled=False))
    attn = paged_attention(
        queries.reshape(tok_rows, heads_here * head_size),
        kv_piece,
        slot_request,
        lax.axis_index("dp"),
    )
    my_ids = lax.dynamic_slice_in_dim(own_ids, tensor_rank * piece_rows, piece_rows, 0)
    spread = jnp.broadcast_to(attn[None], (groups,) + attn.shape)
    heads_all = lax.all_to_all(spread, "tensor", 0, 2, tiled=True).reshape(tok_rows, -1)
    out_cols = out_full.reshape(-1, out_full.shape[3])
    proj = lax.dot_general(
        heads_all, out_cols, (((1,), (1,)), ((), ())), preferred_element_type=jnp.float32
    )
    first = layer_norm(tokens.astype(jnp.float32) + proj).astype(jnp.bfloat16)
    inner = jax.nn.gelu(
        jnp.dot(first, up_block, preferred_element_type=jnp.float32), approximate=False
    ).astype(jnp.bfloat16)
    down_cols = down_block.reshape(-1, down_block.shape[3])
    partial = lax.dot_general(
        inner, down_cols, (((1,), (1,)), ((), ())), preferred_element_type=jnp.float32
    )
    ffn = sum_scatter(partial.astype(jnp.bfloat16))
    first_rows = lax.dynamic_slice_in_dim(first, tensor_rank * piece_rows, piece_rows, 0)
    live = (my_ids >= 0).astype(jnp.float32)[:, None]
    encoded_rows = (layer_norm(first_rows.astype(jnp.float32) + ffn) * live).astype(jnp.bfloat16)
    return gather_rows(encoded_rows)


def solution(mesh):
    in_specs = (
        P("dp", None),
        P(("dp", "tensor"), None),
        P(None, ("dp", "tensor")),
        P(("dp", "tensor"), None),
        P(None, ("dp", "tensor")),
        P(),
    )
    out_specs = P("dp", None)
    return jax.shard_map(shards, mesh=mesh, in_specs=in_specs, out_specs=out_specs, check_vma=False)
```

```python
import math

import jax
import jax.numpy as jnp
from jax import lax
from jax.experimental import pallas as pl
from jax.experimental.pallas import tpu as pltpu
from jax.sharding import PartitionSpec as P

D = 1024
H = 16


def layer_norm(value):
    mean = jnp.mean(value, axis=-1, keepdims=True)
    centred = value - mean
    spread = jnp.mean(centred * centred, axis=-1, keepdims=True)
    return centred * lax.rsqrt(spread + 1e-05)


def spread_weights(w_qkv, w_out, w_up, w_down):
    groups = lax.axis_size("tensor")
    qkv = w_qkv.astype(jnp.bfloat16)
    up = w_up.astype(jnp.bfloat16)
    out_t = w_out.astype(jnp.bfloat16).T
    down_t = w_down.astype(jnp.bfloat16).T
    rows = qkv.shape[0]
    cols = out_t.shape[0]
    parts = [
        qkv.reshape(rows, groups, -1).transpose(1, 0, 2).reshape(groups, -1),
        up.reshape(rows, groups, -1).transpose(1, 0, 2).reshape(groups, -1),
        down_t.reshape(cols, groups, -1).transpose(1, 0, 2).reshape(groups, -1),
        jnp.broadcast_to(out_t.reshape(1, -1), (groups, out_t.size)),
    ]
    sizes = [p.shape[1] for p in parts]
    got = lax.all_to_all(jnp.concatenate(parts, axis=1), "tensor", 0, 0, tiled=True)
    cut = [sum(sizes[:k]) for k in range(5)]
    piece = [got[:, cut[k]:cut[k + 1]] for k in range(4)]
    qkv_local = piece[0].reshape(groups * rows, -1)
    width = up.shape[1] // groups
    up_local = piece[1].reshape(groups * rows, width)
    down_local = piece[2].reshape(-1, width)
    out_local = piece[3].reshape(-1, width)
    qkv_block = lax.all_gather(qkv_local, "dp", axis=0, tiled=True)
    rest = jnp.concatenate([up_local, down_local, out_local], axis=0)
    all_rest = lax.all_gather(rest, "dp", axis=0, tiled=False)
    dp_size = all_rest.shape[0]
    offs = [0, up_local.shape[0], up_local.shape[0] + down_local.shape[0], rest.shape[0]]
    up_block = all_rest[:, offs[0]:offs[1]].reshape(dp_size * up_local.shape[0], width)
    down_full = all_rest[:, offs[1]:offs[2]].reshape(dp_size, groups, cols, -1)
    out_full = all_rest[:, offs[2]:offs[3]].reshape(dp_size, groups, cols, -1)
    return qkv_block, up_block, down_full, out_full


def sum_scatter(part):
    groups = lax.axis_size("tensor")
    pieces = lax.all_to_all(part.reshape(groups, -1, part.shape[1]), "tensor", 0, 0, tiled=True)
    return jnp.sum(pieces.astype(jnp.float32), axis=0)


def gather_rows(rows):
    groups = lax.axis_size("tensor")
    spread = jnp.broadcast_to(rows[None], (groups,) + rows.shape)
    return lax.all_to_all(spread, "tensor", 0, 0, tiled=True).reshape(-1, rows.shape[1])


HEAD = D // H
INTERPRET = False
CHUNK = 24


def attention_kernel(list_ref, count_ref, q_ref, qid_ref, kv_ref, kid_ref, o_ref, m_ref, l_ref, acc_ref):
    i = pl.program_id(0)
    pages = kv_ref.shape[0]
    page = kv_ref.shape[1]
    width = q_ref.shape[1]
    heads = width // HEAD
    scale = 1.0 / math.sqrt(HEAD)
    q = q_ref[...]
    lane_head = lax.broadcasted_iota(jnp.int32, q.shape, 1) // HEAD
    stacked_q = jnp.concatenate(
        [jnp.where(lane_head == h, q, jnp.zeros_like(q)) for h in range(heads)], axis=0
    ) * jnp.asarray(scale, q.dtype)
    qid = qid_ref[...]
    stacked_id = jnp.concatenate([qid] * heads, axis=0)
    count = count_ref[i]
    m_ref[...] = jnp.full(m_ref.shape, -1e30, jnp.float32)
    l_ref[...] = jnp.zeros(l_ref.shape, jnp.float32)
    acc_ref[...] = jnp.zeros(acc_ref.shape, jnp.float32)
    slot_chunk = lax.broadcasted_iota(jnp.int32, (1, CHUNK * page), 1) // page

    def body(c, carry):
        base = c * CHUNK
        kps = [list_ref[i * (pages + CHUNK) + base + j] for j in range(CHUNK)]
        kv = jnp.concatenate([kv_ref[kp] for kp in kps], axis=0)
        k = kv[:, :width]
        v = kv[:, width:]
        kid = jnp.concatenate([kid_ref[kp] for kp in kps], axis=1)
        allowed = stacked_id == kid
        if pages % CHUNK:
            allowed = jnp.logical_and(allowed, slot_chunk + base < count)
        s = lax.dot_general(
            stacked_q, k, (((1,), (1,)), ((), ())), preferred_element_type=jnp.float32
        )
        s = jnp.where(allowed, s, -jnp.inf)
        m_old = m_ref[...]
        m_new = jnp.maximum(m_old, jnp.max(s, axis=1, keepdims=True))
        p = jnp.exp(s - m_new)
        alpha = jnp.exp(m_old - m_new)
        l_ref[...] = alpha * l_ref[...] + jnp.sum(p, axis=1, keepdims=True)
        acc_ref[...] = alpha * acc_ref[...] + jnp.dot(
            p.astype(jnp.bfloat16), v, preferred_element_type=jnp.float32
        )
        m_ref[...] = m_new
        return carry

    lax.fori_loop(0, (count + CHUNK - 1) // CHUNK, body, 0)
    rows = q.shape[0]
    out = acc_ref[0:rows] / l_ref[0:rows]
    for h in range(1, heads):
        out = jnp.where(
            lane_head == h, acc_ref[h * rows:(h + 1) * rows] / l_ref[h * rows:(h + 1) * rows], out
        )
    o_ref[...] = out.astype(o_ref.dtype)


def paged_attention(queries, kv, slot_request, dp_rank):
    pages, page = slot_request.shape
    rows, width = queries.shape
    own_pages = rows // page
    heads = width // HEAD
    present = (
        slot_request[:, :, None] == jnp.arange(-1, 4, dtype=jnp.int32)[None, None, :]
    ).any(axis=1).astype(jnp.float32)
    own = lax.dynamic_slice_in_dim(present, dp_rank * own_pages, own_pages, 0)
    allowed = (jnp.dot(own, present.T) > 0).astype(jnp.int32)
    counts = jnp.sum(allowed, axis=1)
    visit = jnp.argsort(1 - allowed, axis=1, stable=True).astype(jnp.int32)
    visit = jnp.pad(visit, ((0, 0), (0, CHUNK)), mode="edge").reshape(-1)
    own_ids = lax.dynamic_slice_in_dim(slot_request, dp_rank * own_pages, own_pages, 0)
    qid = own_ids.reshape(rows, 1)
    kid = slot_request.reshape(pages, 1, page)
    kv3 = kv.reshape(pages, page, 2 * width)
    grid_spec = pltpu.PrefetchScalarGridSpec(
        num_scalar_prefetch=2,
        grid=(own_pages,),
        in_specs=[
            pl.BlockSpec((page, width), lambda i, a, n: (i, 0)),
            pl.BlockSpec((page, 1), lambda i, a, n: (i, 0)),
            pl.BlockSpec((pages, page, 2 * width), lambda i, a, n: (0, 0, 0)),
            pl.BlockSpec((pages, 1, page), lambda i, a, n: (0, 0, 0)),
        ],
        out_specs=pl.BlockSpec((page, width), lambda i, a, n: (i, 0)),
        scratch_shapes=[
            pltpu.VMEM((heads * page, 1), jnp.float32),
            pltpu.VMEM((heads * page, 1), jnp.float32),
            pltpu.VMEM((heads * page, width), jnp.float32),
        ],
    )
    return pl.pallas_call(
        attention_kernel,
        grid_spec=grid_spec,
        out_shape=jax.ShapeDtypeStruct((rows, width), jnp.bfloat16),
        interpret=INTERPRET,
    )(visit, counts, queries, qid, kv3, kid)


def shards(tokens, w_qkv, w_out, w_up, w_down, slot_request):
    groups = lax.axis_size("tensor")
    tensor_rank = lax.axis_index("tensor")
    qkv_block, up_block, down_block, out_full = spread_weights(w_qkv, w_out, w_up, w_down)
    tok_rows = tokens.shape[0]
    piece_rows = tok_rows // groups
    head_size = D // H
    heads_here = qkv_block.shape[1] // (3 * head_size)
    qkv = jnp.dot(tokens, qkv_block, preferred_element_type=jnp.float32).astype(jnp.bfloat16)
    qkv = qkv.reshape(tok_rows, heads_here, 3, head_size)
    queries = qkv[:, :, 0, :]
    key_rows = qkv[:, :, 1, :].reshape(tok_rows, heads_here * head_size)
    value_rows = qkv[:, :, 2, :].reshape(tok_rows, heads_here * head_size)
    slot_ids = slot_request.reshape(-1)
    own_ids = lax.dynamic_slice_in_dim(slot_ids, lax.axis_index("dp") * tok_rows, tok_rows, 0)

    kv_rows = jnp.concatenate([key_rows, value_rows], axis=1)
    kv_piece = lax.optimization_barrier(lax.all_gather(kv_rows, "dp", axis=0, tiled=False))
    attn = paged_attention(
        queries.reshape(tok_rows, heads_here * head_size),
        kv_piece,
        slot_request,
        lax.axis_index("dp"),
    )
    my_ids = lax.dynamic_slice_in_dim(own_ids, tensor_rank * piece_rows, piece_rows, 0)
    spread = jnp.broadcast_to(attn[None], (groups,) + attn.shape)
    heads_all = lax.all_to_all(spread, "tensor", 0, 2, tiled=True).reshape(tok_rows, -1)
    out_cols = out_full.reshape(-1, out_full.shape[3])
    proj = lax.dot_general(
        heads_all, out_cols, (((1,), (1,)), ((), ())), preferred_element_type=jnp.float32
    )
    first = layer_norm(tokens.astype(jnp.float32) + proj).astype(jnp.bfloat16)
    inner = jax.nn.gelu(
        jnp.dot(first, up_block, preferred_element_type=jnp.float32), approximate=False
    ).astype(jnp.bfloat16)
    down_cols = down_block.reshape(-1, down_block.shape[3])
    partial = lax.dot_general(
        inner, down_cols, (((1,), (1,)), ((), ())), preferred_element_type=jnp.float32
    )
    ffn = sum_scatter(partial.astype(jnp.bfloat16))
    first_rows = lax.dynamic_slice_in_dim(first, tensor_rank * piece_rows, piece_rows, 0)
    live = (my_ids >= 0).astype(jnp.float32)[:, None]
    encoded_rows = (layer_norm(first_rows.astype(jnp.float32) + ffn) * live).astype(jnp.bfloat16)
    return gather_rows(encoded_rows)


def solution(mesh):
    in_specs = (
        P("dp", None),
        P(("dp", "tensor"), None),
        P(None, ("dp", "tensor")),
        P(("dp", "tensor"), None),
        P(None, ("dp", "tensor")),
        P(),
    )
    out_specs = P("dp", None)
    return jax.shard_map(shards, mesh=mesh, in_specs=in_specs, out_specs=out_specs, check_vma=False)
```

```python
import math

import jax
import jax.numpy as jnp
from jax import lax
from jax.experimental import pallas as pl
from jax.experimental.pallas import tpu as pltpu
from jax.sharding import PartitionSpec as P

D = 1024
H = 16


def layer_norm(value):
    mean = jnp.mean(value, axis=-1, keepdims=True)
    centred = value - mean
    spread = jnp.mean(centred * centred, axis=-1, keepdims=True)
    return centred * lax.rsqrt(spread + 1e-05)


def spread_weights(w_qkv, w_out, w_up, w_down):
    groups = lax.axis_size("tensor")
    qkv = w_qkv.astype(jnp.bfloat16)
    up = w_up.astype(jnp.bfloat16)
    out_t = w_out.astype(jnp.bfloat16).T
    down_t = w_down.astype(jnp.bfloat16).T
    rows = qkv.shape[0]
    cols = out_t.shape[0]
    parts = [
        qkv.reshape(rows, groups, -1).transpose(1, 0, 2).reshape(groups, -1),
        up.reshape(rows, groups, -1).transpose(1, 0, 2).reshape(groups, -1),
        down_t.reshape(cols, groups, -1).transpose(1, 0, 2).reshape(groups, -1),
        jnp.broadcast_to(out_t.reshape(1, -1), (groups, out_t.size)),
    ]
    sizes = [p.shape[1] for p in parts]
    got = lax.all_to_all(jnp.concatenate(parts, axis=1), "tensor", 0, 0, tiled=True)
    cut = [sum(sizes[:k]) for k in range(5)]
    piece = [got[:, cut[k]:cut[k + 1]] for k in range(4)]
    qkv_local = piece[0].reshape(groups * rows, -1)
    width = up.shape[1] // groups
    up_local = piece[1].reshape(groups * rows, width)
    down_local = piece[2].reshape(-1, width)
    out_local = piece[3].reshape(-1, width)
    qkv_block = lax.all_gather(qkv_local, "dp", axis=0, tiled=True)
    all_out = lax.all_gather(out_local, "dp", axis=0, tiled=False)
    rest = jnp.concatenate([up_local, down_local], axis=0)
    all_rest = lax.all_gather(rest, "dp", axis=0, tiled=False)
    dp_size = all_rest.shape[0]
    up_rows = up_local.shape[0]
    up_block = all_rest[:, :up_rows].reshape(dp_size * up_rows, width)
    down_full = all_rest[:, up_rows:].reshape(dp_size, groups, cols, -1)
    out_full = all_out.reshape(dp_size, groups, cols, -1)
    return qkv_block, up_block, down_full, out_full


def sum_scatter(part):
    groups = lax.axis_size("tensor")
    pieces = lax.all_to_all(part.reshape(groups, -1, part.shape[1]), "tensor", 0, 0, tiled=True)
    return jnp.sum(pieces.astype(jnp.float32), axis=0)


def gather_rows(rows):
    groups = lax.axis_size("tensor")
    spread = jnp.broadcast_to(rows[None], (groups,) + rows.shape)
    return lax.all_to_all(spread, "tensor", 0, 0, tiled=True).reshape(-1, rows.shape[1])


HEAD = D // H
INTERPRET = False
CHUNK = 24


def attention_kernel(list_ref, count_ref, q_ref, qid_ref, kv_ref, kid_ref, o_ref, m_ref, l_ref, acc_ref):
    i = pl.program_id(0)
    pages = kv_ref.shape[0]
    page = kv_ref.shape[1]
    width = q_ref.shape[1]
    heads = width // HEAD
    scale = 1.0 / math.sqrt(HEAD)
    q = q_ref[...]
    lane_head = lax.broadcasted_iota(jnp.int32, q.shape, 1) // HEAD
    stacked_q = jnp.concatenate(
        [jnp.where(lane_head == h, q, jnp.zeros_like(q)) for h in range(heads)], axis=0
    )
    qid = qid_ref[...]
    stacked_id = jnp.concatenate([qid] * heads, axis=0)
    count = count_ref[i]
    m_ref[...] = jnp.full(m_ref.shape, -1e30, jnp.float32)
    l_ref[...] = jnp.zeros(l_ref.shape, jnp.float32)
    acc_ref[...] = jnp.zeros(acc_ref.shape, jnp.float32)
    slot_chunk = lax.broadcasted_iota(jnp.int32, (1, CHUNK * page), 1) // page

    def body(c, carry):
        base = c * CHUNK
        kps = [list_ref[i * (pages + CHUNK) + base + j] for j in range(CHUNK)]
        kv = jnp.concatenate([kv_ref[kp] for kp in kps], axis=0)
        k = kv[:, :width]
        v = kv[:, width:]
        kid = jnp.concatenate([kid_ref[kp] for kp in kps], axis=1)
        allowed = jnp.logical_and(stacked_id == kid, slot_chunk + base < count)
        s = lax.dot_general(
            stacked_q, k, (((1,), (1,)), ((), ())), preferred_element_type=jnp.float32
        )
        s = jnp.where(allowed, s * scale, -jnp.inf)
        m_old = m_ref[...]
        m_new = jnp.maximum(m_old, jnp.max(s, axis=1, keepdims=True))
        p = jnp.exp(s - m_new)
        alpha = jnp.exp(m_old - m_new)
        l_ref[...] = alpha * l_ref[...] + jnp.sum(p, axis=1, keepdims=True)
        acc_ref[...] = alpha * acc_ref[...] + jnp.dot(
            p.astype(jnp.bfloat16), v, preferred_element_type=jnp.float32
        )
        m_ref[...] = m_new
        return carry

    lax.fori_loop(0, (count + CHUNK - 1) // CHUNK, body, 0)
    rows = q.shape[0]
    out = acc_ref[0:rows] / l_ref[0:rows]
    for h in range(1, heads):
        out = jnp.where(
            lane_head == h, acc_ref[h * rows:(h + 1) * rows] / l_ref[h * rows:(h + 1) * rows], out
        )
    o_ref[...] = out.astype(o_ref.dtype)


def paged_attention(queries, kv, slot_request, dp_rank):
    pages, page = slot_request.shape
    rows, width = queries.shape
    own_pages = rows // page
    heads = width // HEAD
    present = (
        slot_request[:, :, None] == jnp.arange(-1, 4, dtype=jnp.int32)[None, None, :]
    ).any(axis=1).astype(jnp.float32)
    own = lax.dynamic_slice_in_dim(present, dp_rank * own_pages, own_pages, 0)
    allowed = (jnp.dot(own, present.T) > 0).astype(jnp.int32)
    counts = jnp.sum(allowed, axis=1)
    visit = jnp.argsort(1 - allowed, axis=1, stable=True).astype(jnp.int32)
    visit = jnp.pad(visit, ((0, 0), (0, CHUNK)), mode="edge").reshape(-1)
    own_ids = lax.dynamic_slice_in_dim(slot_request, dp_rank * own_pages, own_pages, 0)
    qid = own_ids.reshape(rows, 1)
    kid = slot_request.reshape(pages, 1, page)
    kv3 = kv.reshape(pages, page, 2 * width)
    grid_spec = pltpu.PrefetchScalarGridSpec(
        num_scalar_prefetch=2,
        grid=(own_pages,),
        in_specs=[
            pl.BlockSpec((page, width), lambda i, a, n: (i, 0)),
            pl.BlockSpec((page, 1), lambda i, a, n: (i, 0)),
            pl.BlockSpec((pages, page, 2 * width), lambda i, a, n: (0, 0, 0)),
            pl.BlockSpec((pages, 1, page), lambda i, a, n: (0, 0, 0)),
        ],
        out_specs=pl.BlockSpec((page, width), lambda i, a, n: (i, 0)),
        scratch_shapes=[
            pltpu.VMEM((heads * page, 1), jnp.float32),
            pltpu.VMEM((heads * page, 1), jnp.float32),
            pltpu.VMEM((heads * page, width), jnp.float32),
        ],
    )
    return pl.pallas_call(
        attention_kernel,
        grid_spec=grid_spec,
        out_shape=jax.ShapeDtypeStruct((rows, width), jnp.bfloat16),
        interpret=INTERPRET,
    )(visit, counts, queries, qid, kv3, kid)


def shards(tokens, w_qkv, w_out, w_up, w_down, slot_request):
    groups = lax.axis_size("tensor")
    tensor_rank = lax.axis_index("tensor")
    qkv_block, up_block, down_block, out_full = spread_weights(w_qkv, w_out, w_up, w_down)
    tok_rows = tokens.shape[0]
    piece_rows = tok_rows // groups
    head_size = D // H
    heads_here = qkv_block.shape[1] // (3 * head_size)
    qkv = jnp.dot(tokens, qkv_block, preferred_element_type=jnp.float32).astype(jnp.bfloat16)
    qkv = qkv.reshape(tok_rows, heads_here, 3, head_size)
    queries = qkv[:, :, 0, :]
    key_rows = qkv[:, :, 1, :].reshape(tok_rows, heads_here * head_size)
    value_rows = qkv[:, :, 2, :].reshape(tok_rows, heads_here * head_size)
    slot_ids = slot_request.reshape(-1)
    own_ids = lax.dynamic_slice_in_dim(slot_ids, lax.axis_index("dp") * tok_rows, tok_rows, 0)

    kv_rows = jnp.concatenate([key_rows, value_rows], axis=1)
    kv_piece = lax.optimization_barrier(lax.all_gather(kv_rows, "dp", axis=0, tiled=False))
    attn = paged_attention(
        queries.reshape(tok_rows, heads_here * head_size),
        kv_piece,
        slot_request,
        lax.axis_index("dp"),
    )
    my_ids = lax.dynamic_slice_in_dim(own_ids, tensor_rank * piece_rows, piece_rows, 0)
    spread = jnp.broadcast_to(attn[None], (groups,) + attn.shape)
    heads_all = lax.all_to_all(spread, "tensor", 0, 2, tiled=True).reshape(tok_rows, -1)
    out_cols = out_full.reshape(-1, out_full.shape[3])
    proj = lax.dot_general(
        heads_all, out_cols, (((1,), (1,)), ((), ())), preferred_element_type=jnp.float32
    )
    first = layer_norm(tokens.astype(jnp.float32) + proj).astype(jnp.bfloat16)
    inner = jax.nn.gelu(
        jnp.dot(first, up_block, preferred_element_type=jnp.float32), approximate=False
    ).astype(jnp.bfloat16)
    down_cols = down_block.reshape(-1, down_block.shape[3])
    partial = lax.dot_general(
        inner, down_cols, (((1,), (1,)), ((), ())), preferred_element_type=jnp.float32
    )
    ffn = sum_scatter(partial.astype(jnp.bfloat16))
    first_rows = lax.dynamic_slice_in_dim(first, tensor_rank * piece_rows, piece_rows, 0)
    live = (my_ids >= 0).astype(jnp.float32)[:, None]
    encoded_rows = (layer_norm(first_rows.astype(jnp.float32) + ffn) * live).astype(jnp.bfloat16)
    return gather_rows(encoded_rows)


def solution(mesh):
    in_specs = (
        P("dp", None),
        P(("dp", "tensor"), None),
        P(None, ("dp", "tensor")),
        P(("dp", "tensor"), None),
        P(None, ("dp", "tensor")),
        P(),
    )
    out_specs = P("dp", None)
    return jax.shard_map(shards, mesh=mesh, in_specs=in_specs, out_specs=out_specs, check_vma=False)
```

```python
import math

import jax
import jax.numpy as jnp
from jax import lax
from jax.experimental import pallas as pl
from jax.experimental.pallas import tpu as pltpu
from jax.sharding import PartitionSpec as P

D = 1024
H = 16


def layer_norm(value):
    mean = jnp.mean(value, axis=-1, keepdims=True)
    centred = value - mean
    spread = jnp.mean(centred * centred, axis=-1, keepdims=True)
    return centred * lax.rsqrt(spread + 1e-05)


def spread_weights(w_qkv, w_out, w_up, w_down):
    groups = lax.axis_size("tensor")
    qkv = w_qkv.astype(jnp.bfloat16)
    up = w_up.astype(jnp.bfloat16)
    out_t = w_out.astype(jnp.bfloat16).T
    down_t = w_down.astype(jnp.bfloat16).T
    rows = qkv.shape[0]
    cols = out_t.shape[0]
    parts = [
        qkv.reshape(rows, groups, -1).transpose(1, 0, 2).reshape(groups, -1),
        up.reshape(rows, groups, -1).transpose(1, 0, 2).reshape(groups, -1),
        down_t.reshape(cols, groups, -1).transpose(1, 0, 2).reshape(groups, -1),
        jnp.broadcast_to(out_t.reshape(1, -1), (groups, out_t.size)),
    ]
    sizes = [p.shape[1] for p in parts]
    got = lax.all_to_all(jnp.concatenate(parts, axis=1), "tensor", 0, 0, tiled=True)
    cut = [sum(sizes[:k]) for k in range(5)]
    piece = [got[:, cut[k]:cut[k + 1]] for k in range(4)]
    qkv_local = piece[0].reshape(groups * rows, -1)
    width = up.shape[1] // groups
    up_local = piece[1].reshape(groups * rows, width)
    down_local = piece[2].reshape(-1, width)
    out_local = piece[3].reshape(-1, width)
    qkv_block = lax.all_gather(qkv_local, "dp", axis=0, tiled=True)
    rest = jnp.concatenate([up_local, down_local, out_local], axis=0)
    all_rest = lax.all_gather(rest, "dp", axis=0, tiled=False)
    dp_size = all_rest.shape[0]
    offs = [0, up_local.shape[0], up_local.shape[0] + down_local.shape[0], rest.shape[0]]
    up_block = all_rest[:, offs[0]:offs[1]].reshape(dp_size * up_local.shape[0], width)
    down_full = all_rest[:, offs[1]:offs[2]].reshape(dp_size, groups, cols, -1)
    out_full = all_rest[:, offs[2]:offs[3]].reshape(dp_size, groups, cols, -1)
    return qkv_block, up_block, down_full, out_full


def sum_scatter(part):
    groups = lax.axis_size("tensor")
    pieces = lax.all_to_all(part.reshape(groups, -1, part.shape[1]), "tensor", 0, 0, tiled=True)
    return jnp.sum(pieces.astype(jnp.float32), axis=0)


def gather_rows(rows):
    groups = lax.axis_size("tensor")
    spread = jnp.broadcast_to(rows[None], (groups,) + rows.shape)
    return lax.all_to_all(spread, "tensor", 0, 0, tiled=True).reshape(-1, rows.shape[1])


HEAD = D // H
INTERPRET = False
CHUNK = 20


def attention_kernel(list_ref, count_ref, q_ref, qid_ref, kv_ref, kid_ref, o_ref, m_ref, l_ref, acc_ref):
    i = pl.program_id(0)
    pages = kv_ref.shape[0]
    page = kv_ref.shape[1]
    width = q_ref.shape[1]
    heads = width // HEAD
    scale = 1.0 / math.sqrt(HEAD)
    q = q_ref[...]
    lane_head = lax.broadcasted_iota(jnp.int32, q.shape, 1) // HEAD
    stacked_q = jnp.concatenate(
        [jnp.where(lane_head == h, q, jnp.zeros_like(q)) for h in range(heads)], axis=0
    )
    qid = qid_ref[...]
    stacked_id = jnp.concatenate([qid] * heads, axis=0)
    count = count_ref[i]
    m_ref[...] = jnp.full(m_ref.shape, -1e30, jnp.float32)
    l_ref[...] = jnp.zeros(l_ref.shape, jnp.float32)
    acc_ref[...] = jnp.zeros(acc_ref.shape, jnp.float32)
    slot_chunk = lax.broadcasted_iota(jnp.int32, (1, CHUNK * page), 1) // page

    def body(c, carry):
        base = c * CHUNK
        kps = [list_ref[i * (pages + CHUNK) + base + j] for j in range(CHUNK)]
        kv = jnp.concatenate([kv_ref[kp] for kp in kps], axis=0)
        k = kv[:, :width]
        v = kv[:, width:]
        kid = jnp.concatenate([kid_ref[kp] for kp in kps], axis=1)
        allowed = jnp.logical_and(stacked_id == kid, slot_chunk + base < count)
        s = lax.dot_general(
            stacked_q, k, (((1,), (1,)), ((), ())), preferred_element_type=jnp.float32
        )
        s = jnp.where(allowed, s * scale, -jnp.inf)
        m_old = m_ref[...]
        m_new = jnp.maximum(m_old, jnp.max(s, axis=1, keepdims=True))
        p = jnp.exp(s - m_new)
        alpha = jnp.exp(m_old - m_new)
        l_ref[...] = alpha * l_ref[...] + jnp.sum(p, axis=1, keepdims=True)
        acc_ref[...] = alpha * acc_ref[...] + jnp.dot(
            p.astype(jnp.bfloat16), v, preferred_element_type=jnp.float32
        )
        m_ref[...] = m_new
        return carry

    lax.fori_loop(0, (count + CHUNK - 1) // CHUNK, body, 0)
    rows = q.shape[0]
    out = acc_ref[0:rows] / l_ref[0:rows]
    for h in range(1, heads):
        out = jnp.where(
            lane_head == h, acc_ref[h * rows:(h + 1) * rows] / l_ref[h * rows:(h + 1) * rows], out
        )
    o_ref[...] = out.astype(o_ref.dtype)


def paged_attention(queries, kv, slot_request, dp_rank):
    pages, page = slot_request.shape
    rows, width = queries.shape
    own_pages = rows // page
    heads = width // HEAD
    present = (
        slot_request[:, :, None] == jnp.arange(-1, 4, dtype=jnp.int32)[None, None, :]
    ).any(axis=1).astype(jnp.float32)
    own = lax.dynamic_slice_in_dim(present, dp_rank * own_pages, own_pages, 0)
    allowed = (jnp.dot(own, present.T) > 0).astype(jnp.int32)
    counts = jnp.sum(allowed, axis=1)
    visit = jnp.argsort(1 - allowed, axis=1, stable=True).astype(jnp.int32)
    visit = jnp.pad(visit, ((0, 0), (0, CHUNK)), mode="edge").reshape(-1)
    own_ids = lax.dynamic_slice_in_dim(slot_request, dp_rank * own_pages, own_pages, 0)
    qid = own_ids.reshape(rows, 1)
    kid = slot_request.reshape(pages, 1, page)
    kv3 = kv.reshape(pages, page, 2 * width)
    grid_spec = pltpu.PrefetchScalarGridSpec(
        num_scalar_prefetch=2,
        grid=(own_pages,),
        in_specs=[
            pl.BlockSpec((page, width), lambda i, a, n: (i, 0)),
            pl.BlockSpec((page, 1), lambda i, a, n: (i, 0)),
            pl.BlockSpec((pages, page, 2 * width), lambda i, a, n: (0, 0, 0)),
            pl.BlockSpec((pages, 1, page), lambda i, a, n: (0, 0, 0)),
        ],
        out_specs=pl.BlockSpec((page, width), lambda i, a, n: (i, 0)),
        scratch_shapes=[
            pltpu.VMEM((heads * page, 1), jnp.float32),
            pltpu.VMEM((heads * page, 1), jnp.float32),
            pltpu.VMEM((heads * page, width), jnp.float32),
        ],
    )
    return pl.pallas_call(
        attention_kernel,
        grid_spec=grid_spec,
        out_shape=jax.ShapeDtypeStruct((rows, width), jnp.bfloat16),
        interpret=INTERPRET,
    )(visit, counts, queries, qid, kv3, kid)


def shards(tokens, w_qkv, w_out, w_up, w_down, slot_request):
    groups = lax.axis_size("tensor")
    tensor_rank = lax.axis_index("tensor")
    qkv_block, up_block, down_block, out_full = spread_weights(w_qkv, w_out, w_up, w_down)
    tok_rows = tokens.shape[0]
    piece_rows = tok_rows // groups
    head_size = D // H
    heads_here = qkv_block.shape[1] // (3 * head_size)
    qkv = jnp.dot(tokens, qkv_block, preferred_element_type=jnp.float32).astype(jnp.bfloat16)
    qkv = qkv.reshape(tok_rows, heads_here, 3, head_size)
    queries = qkv[:, :, 0, :]
    key_rows = qkv[:, :, 1, :].reshape(tok_rows, heads_here * head_size)
    value_rows = qkv[:, :, 2, :].reshape(tok_rows, heads_here * head_size)
    slot_ids = slot_request.reshape(-1)
    own_ids = lax.dynamic_slice_in_dim(slot_ids, lax.axis_index("dp") * tok_rows, tok_rows, 0)

    kv_rows = jnp.concatenate([key_rows, value_rows], axis=1)
    kv_piece = lax.optimization_barrier(lax.all_gather(kv_rows, "dp", axis=0, tiled=False))
    attn = paged_attention(
        queries.reshape(tok_rows, heads_here * head_size),
        kv_piece,
        slot_request,
        lax.axis_index("dp"),
    )
    my_ids = lax.dynamic_slice_in_dim(own_ids, tensor_rank * piece_rows, piece_rows, 0)
    spread = jnp.broadcast_to(attn[None], (groups,) + attn.shape)
    heads_all = lax.all_to_all(spread, "tensor", 0, 2, tiled=True).reshape(tok_rows, -1)
    out_cols = out_full.reshape(-1, out_full.shape[3])
    proj = lax.dot_general(
        heads_all, out_cols, (((1,), (1,)), ((), ())), preferred_element_type=jnp.float32
    )
    first = layer_norm(tokens.astype(jnp.float32) + proj).astype(jnp.bfloat16)
    inner = jax.nn.gelu(
        jnp.dot(first, up_block, preferred_element_type=jnp.float32), approximate=False
    ).astype(jnp.bfloat16)
    down_cols = down_block.reshape(-1, down_block.shape[3])
    partial = lax.dot_general(
        inner, down_cols, (((1,), (1,)), ((), ())), preferred_element_type=jnp.float32
    )
    ffn = sum_scatter(partial.astype(jnp.bfloat16))
    first_rows = lax.dynamic_slice_in_dim(first, tensor_rank * piece_rows, piece_rows, 0)
    live = (my_ids >= 0).astype(jnp.float32)[:, None]
    encoded_rows = (layer_norm(first_rows.astype(jnp.float32) + ffn) * live).astype(jnp.bfloat16)
    return gather_rows(encoded_rows)


def solution(mesh):
    in_specs = (
        P("dp", None),
        P(("dp", "tensor"), None),
        P(None, ("dp", "tensor")),
        P(("dp", "tensor"), None),
        P(None, ("dp", "tensor")),
        P(),
    )
    out_specs = P("dp", None)
    return jax.shard_map(shards, mesh=mesh, in_specs=in_specs, out_specs=out_specs, check_vma=False)
```
